512 devices in a mesh: seq: 32 (over y, x), tp: 16 (over z, core).
Axes of the slice: x: 4, y: 8, z: 8, core: 2. Of those that a mesh axis runs over, the one named last changes fastest.
Arguments:
- segment_ids: int32 [8192], replicated, may hold values from 0 to 15, never falling along the last dimension, each value on 1 to 2048 neighbouring positions
- relayout: int32 [8192], replicated, may hold values from 0 to 8191, as said below
- queries: bfloat16 [8192, 4096], P('seq', 'tp'), may hold values from -8 to 8
- keys: bfloat16 [8192, 512], P(('seq', 'tp')), may hold values from -8 to 8
- values: bfloat16 [8192, 512], P(('seq', 'tp')), may hold values from -18 to 18
- out_weight: bfloat16 [4096, 8192], P('tp'), may hold values from -0.09375 to 0.09375
Outputs:
- block_out: bfloat16 [8192, 8192], P(('seq', 'tp'))
The draws below stay inside these ranges and needn't reach their ends.
Inputs may be any that keep to these rules, and one draw needn't show every extreme that they name: relayout is a permutation; of the 256 tokens in each aligned block of 256 initial positions exactly 8 land in each aligned block of 256 new positions.
All inputs are finite; a program needn't handle non-finite values.
Results may differ from the reference program's by a relative error of at most 0.017.
Values may be sent and summed in bfloat16 or wider, within the bound.
No kernel may reach another device: no remote copies, remote signals or barrier semaphores. Data moves between devices by JAX's collectives and lax.ppermute only.
A program may use at most 64 MiB of HBM per device.

```python
import math
import jax
import jax.numpy as jnp
import numpy as np
from jax import lax

D = 8192
QH = 32
KVH = 4
HD = 128
TOK_DEV = 256
TOKENS = 8192
MOST_LEN = 2048
DOCS = 16
N_TP = 16


def query_key_pair(key):
    base = jax.random.fold_in(key, 11)
    key_query, key_key = jax.random.split(base, 2)
    query_draw = jax.random.normal(key_query, (TOKENS, QH * HD), jnp.float32)
    key_draw = jax.random.normal(key_key, (TOKENS, KVH * HD), jnp.float32)
    return (jnp.clip(query_draw, -8.0, 8.0), jnp.clip(key_draw, -8.0, 8.0))


def draw_queries(key, part):
    return query_key_pair(key)[0].astype(jnp.bfloat16)


def draw_keys(key, part):
    return query_key_pair(key)[1].astype(jnp.bfloat16)


def draw_relayout(key, part):
    base = jax.random.fold_in(key, 23)
    key_first, key_second = jax.random.split(base, 2)
    positions = jnp.arange(TOKENS, dtype=jnp.int32)
    blocks = TOKENS // TOK_DEV
    source = positions // TOK_DEV
    shuffle_first = jax.random.permutation(key_first, TOKENS).astype(jnp.int32)
    order = jnp.argsort(source * TOKENS + shuffle_first)
    ranks = jnp.zeros((TOKENS,), jnp.int32).at[order].set(positions % TOK_DEV)
    target = ranks % blocks
    shuffle_second = jax.random.permutation(key_second, TOKENS).astype(jnp.int32)
    return jnp.argsort(target * TOKENS + shuffle_second).astype(jnp.int32)


def level_of(rng, extent, shards, smallest, high):
    factor_of, own = 1.0, jax.random.fold_in(rng, 6)
    for position, parts in shards:
        heights = jnp.exp(jax.random.uniform(jax.random.fold_in(own, position), (parts,), jnp.float32, smallest / len(shards), high / len(shards)))
        factor_of = factor_of * jnp.repeat(heights, extent[position] // parts).reshape([-1 if axis == position else 1 for axis in range(len(extent))])
    return factor_of


def split_up(count, total, most, lean):
    loads = [(1 << 20) // math.isqrt(grade ** lean) + 1 for grade in range(2, count + 1)]
    rest, given = total - most - (count - 1), [1] * (count - 1)
    while rest > 0:
        candidates = [i for i in range(count - 1) if given[i] < most]
        mass, budget = sum([loads[i] for i in candidates]), rest
        for i in candidates:
            addition = min(most - given[i], max(1, budget * loads[i] // mass), rest)
            given[i] = given[i] + addition
            rest = rest - addition
    return np.array([most] + given)


def uneven_parts(own_key, amount, total, most, lean):
    if amount == 2:
        one = jax.random.randint(own_key, (), max(1, total - most), min(most, total - 1) + 1)
        return jnp.stack([one, total - one])
    sizes = jnp.asarray(split_up(amount, total, most, lean), jnp.int32)
    twos = (amount - 1) // 2
    source_of, sink = sizes[1:1 + 2 * twos:2], sizes[2:2 + 2 * twos:2]
    margin = jnp.minimum(source_of - 1, most - sink)
    moved = jax.random.randint(jax.random.fold_in(own_key, 1), (twos,), 0, 1 << 20) % (margin + 1)
    sizes = sizes.at[1:1 + 2 * twos:2].set(source_of - moved).at[2:2 + 2 * twos:2].set(sink + moved)
    return sizes[jax.random.permutation(jax.random.fold_in(own_key, 2), amount)]


def noise(own_key, dims, scale, most, cuts=(), kind=jnp.bfloat16):
    array = jax.random.normal(own_key, dims, jnp.float32) * scale
    if len(cuts) > 0:
        array = level_of(own_key, dims, cuts, -0.22, 0.18) * array
    return jnp.clip(array, min=-most, max=most).astype(kind)


def setup_inputs(seed: int = 0) -> dict:
    splits = jax.random.split(jax.random.key(seed), 7)
    segment_ids = jnp.searchsorted(jnp.cumsum(uneven_parts(splits[0], DOCS, TOKENS, MOST_LEN, 1)), jnp.arange(TOKENS), side="right").astype(jnp.int32)
    relayout = draw_relayout(jax.random.fold_in(splits[6], 71), 0)
    queries = draw_queries(jax.random.fold_in(splits[6], 71), 0)
    keys = draw_keys(jax.random.fold_in(splits[6], 71), 0)
    values = noise(splits[4], (TOKENS, KVH * HD), 3.0, 18.0, ((0, 512),))
    out_weight = noise(splits[5], (QH * HD, D), (QH * HD) ** -0.5, 0.09375, ((0, 16),))
    return {"segment_ids": segment_ids, "relayout": relayout, "queries": queries, "keys": keys, "values": values, "out_weight": out_weight}


def reference(segment_ids, relayout, queries, keys, values, out_weight):
    group = QH // KVH
    block = math.gcd(TOKENS, 512)
    reach = MOST_LEN
    scale = HD ** -0.5
    query_heads = queries.reshape(TOKENS, KVH, group, HD)
    key_pad = jnp.concatenate([jnp.zeros((reach, KVH * HD), jnp.bfloat16), keys], axis=0).reshape(TOKENS + reach, KVH, HD)
    value_pad = jnp.concatenate([jnp.zeros((reach, KVH * HD), jnp.bfloat16), values], axis=0).reshape(TOKENS + reach, KVH, HD)
    seg_pad = jnp.concatenate([jnp.full((reach,), -1, jnp.int32), segment_ids], axis=0)

    def one_block(index):
        start = (index * block).astype(jnp.int32)
        q_block = lax.dynamic_slice_in_dim(query_heads, start, block, 0).astype(jnp.float32)
        k_block = lax.dynamic_slice_in_dim(key_pad, start, reach + block, 0).astype(jnp.float32)
        v_block = lax.dynamic_slice_in_dim(value_pad, start, reach + block, 0).astype(jnp.float32)
        q_pos = start + jnp.arange(block, dtype=jnp.int32)
        q_seg = lax.dynamic_slice_in_dim(segment_ids, start, block, 0)
        k_pos = start - reach + jnp.arange(reach + block, dtype=jnp.int32)
        k_seg = lax.dynamic_slice_in_dim(seg_pad, start, reach + block, 0)
        live = (k_pos[None, :] <= q_pos[:, None]) & (k_seg[None, :] == q_seg[:, None]) & (k_pos[None, :] >= 0)
        scores = jnp.einsum("qngd,knd->ngqk", q_block, k_block) * scale
        masked = jnp.where(live, scores, jnp.float32(-1e30))
        peak = jnp.max(masked, axis=-1, keepdims=True)
        expo = jnp.where(live, jnp.exp(masked - peak), jnp.float32(0.0))
        denom = jnp.sum(expo, axis=-1)
        weight = lax.optimization_barrier(expo.astype(jnp.bfloat16)).astype(jnp.float32)
        summed = jnp.einsum("ngqk,knd->ngqd", weight, v_block)
        attn = summed / denom[..., None]
        return jnp.transpose(attn, (2, 0, 1, 3)).reshape(block, QH * HD).astype(jnp.bfloat16)

    attn_all = lax.map(one_block, jnp.arange(TOKENS // block, dtype=jnp.int32)).reshape(TOKENS, QH * HD)
    relaid = attn_all[relayout]
    width = QH * HD // N_TP
    result = jnp.zeros((TOKENS, D), jnp.float32)
    for group_index in range(N_TP):
        part = jnp.dot(relaid[:, group_index * width:(group_index + 1) * width], out_weight[group_index * width:(group_index + 1) * width], preferred_element_type=jnp.float32)
        result = result + part.astype(jnp.bfloat16).astype(jnp.float32)
    return result.astype(jnp.bfloat16)
```

```python
import jax
import jax.numpy as jnp
import numpy as np
from jax import lax
from jax.sharding import Mesh
from jax.sharding import PartitionSpec as P

QH = 32
KVH = 4
HD = 128
MOST_LEN = 2048


def shards(segment_ids, relayout, queries, keys, values, out_weight):
    rows = queries.shape[0]
    n_seq = lax.axis_size("seq")
    n_z = lax.axis_size("z")
    n_core = lax.axis_size("core")
    s = lax.axis_index("seq")
    t = lax.axis_index("z") * n_core + lax.axis_index("core")
    heads_here = queries.shape[1] // HD
    group = QH // KVH
    kv_width = keys.shape[1]
    scale = HD ** (-0.5)
    back = -(-(MOST_LEN - 1) // rows)
    back = min(back, n_seq - 1)

    kv = jnp.concatenate([keys, values], axis=1)
    kv_block = lax.all_gather(kv, ("z", "core"), axis=0, tiled=True)
    g = t * heads_here // group
    own_k = lax.dynamic_slice_in_dim(kv_block, g * HD, HD, 1)
    own_v = lax.dynamic_slice_in_dim(kv_block, kv_width + g * HD, HD, 1)
    own = jnp.concatenate([own_k, own_v], axis=1)

    window = []
    for k in range(back, 0, -1):
        window.append(
            lax.ppermute(own, "seq", perm=[(i, i + k) for i in range(n_seq - k)])
        )
    window.append(own)
    kv_win = jnp.concatenate(window, axis=0)
    n_keys = kv_win.shape[0]
    k_win = kv_win[:, :HD]
    v_win = kv_win[:, HD:]

    q_pos = s * rows + jnp.arange(rows, dtype=jnp.int32)
    k_pos = (s - back) * rows + jnp.arange(n_keys, dtype=jnp.int32)
    q_seg = lax.dynamic_slice_in_dim(segment_ids, s * rows, rows, 0)
    k_seg = jnp.take(segment_ids, jnp.clip(k_pos, 0, segment_ids.shape[0] - 1))
    live = (
        (k_pos[None, :] <= q_pos[:, None])
        & (k_seg[None, :] == q_seg[:, None])
        & (k_pos[None, :] >= 0)
    )

    q = queries.reshape(rows, heads_here, HD)
    scores = jnp.einsum("qhd,kd->hqk", q, k_win, preferred_element_type=jnp.float32) * scale
    masked = jnp.where(live[None], scores, jnp.float32(-1e30))
    peak = jnp.max(masked, axis=-1)
    expo = jnp.where(live[None], jnp.exp(masked - peak[..., None]), jnp.float32(0.0))
    denom = jnp.sum(expo, axis=-1)
    summed = jnp.einsum(
        "hqk,kd->hqd", expo.astype(jnp.bfloat16), v_win, preferred_element_type=jnp.float32
    )
    attn = summed / denom[..., None]
    attn_rows = jnp.transpose(attn, (1, 0, 2)).reshape(rows, heads_here * HD).astype(jnp.bfloat16)

    chunk = rows // n_seq
    total = relayout.shape[0]
    here = s * rows + jnp.arange(rows, dtype=jnp.int32)
    new_of = jnp.sum(
        jnp.where(relayout[None, :] == here[:, None], jnp.arange(total, dtype=jnp.int32)[None, :], 0),
        axis=1,
    )
    rank = jnp.sum((new_of[None, :] < new_of[:, None]).astype(jnp.int32), axis=1)
    send_sel = (rank[None, :] == jnp.arange(rows, dtype=jnp.int32)[:, None]).astype(jnp.bfloat16)
    to_send = jnp.dot(send_sel, attn_rows, preferred_element_type=jnp.float32).astype(jnp.bfloat16)
    arrived = lax.all_to_all(to_send, "seq", split_axis=0, concat_axis=0, tiled=True)

    src = lax.dynamic_slice_in_dim(relayout, s * rows, rows, 0) // rows
    before = jnp.arange(rows)[None, :] < jnp.arange(rows)[:, None]
    nth = jnp.sum((before & (src[None, :] == src[:, None])).astype(jnp.int32), axis=1)
    slot = src * chunk + nth
    per_dev = rows // (n_z * n_core)
    r = jnp.arange(rows, dtype=jnp.int32)
    c_of = r // (n_z * per_dev)
    z_of = (r // per_dev) % n_z
    m_of = r % per_dev
    q_of = (z_of * n_core + c_of) * per_dev + m_of
    slot_of = jnp.take(slot, q_of)
    recv_sel = (slot_of[:, None] == jnp.arange(rows, dtype=jnp.int32)[None, :]).astype(jnp.bfloat16)
    relaid = jnp.dot(recv_sel, arrived, preferred_element_type=jnp.float32).astype(jnp.bfloat16)

    part = jnp.dot(relaid, out_weight, preferred_element_type=jnp.float32).astype(jnp.bfloat16)
    half = lax.psum_scatter(part, "core", scatter_dimension=0, tiled=True)
    return lax.psum_scatter(half, "z", scatter_dimension=0, tiled=True)


def solution(mesh):
    n_seq, n_tp = mesh.devices.shape
    mesh3 = Mesh(mesh.devices.reshape(n_seq, n_tp // 2, 2), ("seq", "z", "core"))
    tp = ("z", "core")
    return jax.shard_map(
        shards,
        mesh=mesh3,
        in_specs=(
            P(),
            P(),
            P("seq", tp),
            P(("seq",) + tp, None),
            P(("seq",) + tp, None),
            P(tp, None),
        ),
        out_specs=P(("seq",) + tp, None),
        check_vma=False,
    )
```

```python
import jax
import jax.numpy as jnp
import numpy as np
from jax import lax
from jax.sharding import Mesh
from jax.sharding import PartitionSpec as P

QH = 32
KVH = 4
HD = 128
MOST_LEN = 2048


def shards(segment_ids, relayout, queries, keys, values, out_weight):
    rows = queries.shape[0]
    n_seq = lax.axis_size("y") * lax.axis_size("x")
    n_z = lax.axis_size("z")
    n_core = lax.axis_size("core")
    s = lax.axis_index("y") * lax.axis_size("x") + lax.axis_index("x")
    t = lax.axis_index("z") * n_core + lax.axis_index("core")
    heads_here = queries.shape[1] // HD
    group = QH // KVH
    kv_width = keys.shape[1]
    scale = HD ** (-0.5)
    back = -(-(MOST_LEN - 1) // rows)
    back = min(back, n_seq - 1)

    kv = jnp.concatenate([keys, values], axis=1)
    kv_pair = lax.all_gather(kv, "core", axis=0, tiled=True)
    kv_block = lax.all_gather(kv_pair, "z", axis=0, tiled=True)
    g = t * heads_here // group
    own_k = lax.dynamic_slice_in_dim(kv_block, g * HD, HD, 1)
    own_v = lax.dynamic_slice_in_dim(kv_block, kv_width + g * HD, HD, 1)
    own = jnp.concatenate([own_k, own_v], axis=1)

    n_x = lax.axis_size("x")
    n_y = lax.axis_size("y")
    x = lax.axis_index("x")
    row = lax.all_gather(own, "x", axis=0, tiled=True)
    rows_back = -(-back // n_x)
    window = []
    for k in range(rows_back, 0, -1):
        window.append(lax.ppermute(row, "y", perm=[(i, i + k) for i in range(n_y - k)]))
    window.append(row)
    kv_all = jnp.concatenate(window, axis=0)
    n_keys = (back + 1) * rows
    first = (rows_back * n_x - back + x) * rows
    kv_win = lax.dynamic_slice_in_dim(kv_all, first, n_keys, 0)
    k_win = kv_win[:, :HD]
    v_win = kv_win[:, HD:]

    q_pos = s * rows + jnp.arange(rows, dtype=jnp.int32)
    k_pos = (s - back) * rows + jnp.arange(n_keys, dtype=jnp.int32)
    q_seg = lax.dynamic_slice_in_dim(segment_ids, s * rows, rows, 0)
    seg_pad = jnp.concatenate([jnp.full((back * rows,), -1, jnp.int32), segment_ids])
    k_seg = lax.dynamic_slice_in_dim(seg_pad, s * rows, n_keys, 0)
    live = (
        (k_pos[None, :] <= q_pos[:, None])
        & (k_seg[None, :] == q_seg[:, None])
        & (k_pos[None, :] >= 0)
    )

    q = queries.reshape(rows, heads_here, HD)
    scores = jnp.einsum("qhd,kd->hqk", q, k_win, preferred_element_type=jnp.float32) * scale
    masked = jnp.where(live[None], scores, jnp.float32(-1e30))
    peak = jnp.max(masked, axis=-1)
    expo = jnp.where(live[None], jnp.exp(masked - peak[..., None]), jnp.float32(0.0))
    denom = jnp.sum(expo, axis=-1)
    summed = jnp.einsum(
        "hqk,kd->hqd", expo.astype(jnp.bfloat16), v_win, preferred_element_type=jnp.float32
    )
    attn = summed / denom[..., None]
    attn_rows = jnp.transpose(attn, (1, 0, 2)).reshape(rows, heads_here * HD).astype(jnp.bfloat16)

    chunk = rows // n_seq
    total = relayout.shape[0]
    here = s * rows + jnp.arange(rows, dtype=jnp.int32)
    new_of = jnp.sum(
        jnp.where(relayout[None, :] == here[:, None], jnp.arange(total, dtype=jnp.int32)[None, :], 0),
        axis=1,
    )
    rank = jnp.sum((new_of[None, :] < new_of[:, None]).astype(jnp.int32), axis=1)
    send_sel = (rank[None, :] == jnp.arange(rows, dtype=jnp.int32)[:, None]).astype(jnp.bfloat16)
    to_send = jnp.dot(send_sel, attn_rows, preferred_element_type=jnp.float32).astype(jnp.bfloat16)
    arrived = lax.all_to_all(to_send, ("y", "x"), split_axis=0, concat_axis=0, tiled=True)

    src = lax.dynamic_slice_in_dim(relayout, s * rows, rows, 0) // rows
    before = jnp.arange(rows)[None, :] < jnp.arange(rows)[:, None]
    nth = jnp.sum((before & (src[None, :] == src[:, None])).astype(jnp.int32), axis=1)
    slot = src * chunk + nth
    per_dev = rows // (n_z * n_core)
    slot_of = jnp.transpose(slot.reshape(n_z, n_core, per_dev), (1, 0, 2)).reshape(rows)
    recv_sel = (slot_of[:, None] == jnp.arange(rows, dtype=jnp.int32)[None, :]).astype(jnp.bfloat16)
    relaid = jnp.dot(recv_sel, arrived, preferred_element_type=jnp.float32).astype(jnp.bfloat16)

    part = jnp.dot(relaid, out_weight, preferred_element_type=jnp.float32).astype(jnp.bfloat16)
    half = lax.psum_scatter(part, "core", scatter_dimension=0, tiled=True)
    return lax.psum_scatter(half, "z", scatter_dimension=0, tiled=True)


def solution(mesh):
    n_seq, n_tp = mesh.devices.shape
    n_x = 4
    mesh4 = Mesh(mesh.devices.reshape(n_seq // n_x, n_x, n_tp // 2, 2), ("y", "x", "z", "core"))
    seq = ("y", "x")
    tp = ("z", "core")
    return jax.shard_map(
        shards,
        mesh=mesh4,
        in_specs=(
            P(),
            P(),
            P(seq, tp),
            P(seq + tp, None),
            P(seq + tp, None),
            P(tp, None),
        ),
        out_specs=P(seq + tp, None),
        check_vma=False,
    )
```

```python
import jax
import jax.numpy as jnp
import numpy as np
from jax import lax
from jax.sharding import Mesh
from jax.sharding import PartitionSpec as P

QH = 32
KVH = 4
HD = 128
MOST_LEN = 2048


def shards(segment_ids, relayout, queries, keys, values, out_weight):
    rows = queries.shape[0]
    n_seq = lax.axis_size("y") * lax.axis_size("x")
    n_z = lax.axis_size("z")
    n_core = lax.axis_size("core")
    s = lax.axis_index("y") * lax.axis_size("x") + lax.axis_index("x")
    t = lax.axis_index("z") * n_core + lax.axis_index("core")
    heads_here = queries.shape[1] // HD
    group = QH // KVH
    kv_width = keys.shape[1]
    scale = HD ** (-0.5)
    back = -(-(MOST_LEN - 1) // rows)
    back = min(back, n_seq - 1)

    kv = jnp.concatenate([keys, values], axis=1)
    kv_block = lax.all_gather(kv, ("z", "core"), axis=0, tiled=True)
    g = t * heads_here // group
    own_k = lax.dynamic_slice_in_dim(kv_block, g * HD, HD, 1)
    own_v = lax.dynamic_slice_in_dim(kv_block, kv_width + g * HD, HD, 1)
    own = jnp.concatenate([own_k, own_v], axis=1)

    n_x = lax.axis_size("x")
    n_y = lax.axis_size("y")
    x = lax.axis_index("x")
    row = lax.all_gather(own, "x", axis=0, tiled=True)
    rows_back = -(-back // n_x)
    window = []
    for k in range(rows_back, 0, -1):
        window.append(lax.ppermute(row, "y", perm=[(i, i + k) for i in range(n_y - k)]))
    window.append(row)
    kv_all = jnp.concatenate(window, axis=0)
    n_keys = (back + 1) * rows
    first = (rows_back * n_x - back + x) * rows
    kv_win = lax.dynamic_slice_in_dim(kv_all, first, n_keys, 0)
    k_win = kv_win[:, :HD]
    v_win = kv_win[:, HD:]

    q_pos = s * rows + jnp.arange(rows, dtype=jnp.int32)
    k_pos = (s - back) * rows + jnp.arange(n_keys, dtype=jnp.int32)
    q_seg = lax.dynamic_slice_in_dim(segment_ids, s * rows, rows, 0)
    seg_pad = jnp.concatenate([jnp.full((back * rows,), -1, jnp.int32), segment_ids])
    k_seg = lax.dynamic_slice_in_dim(seg_pad, s * rows, n_keys, 0)
    live = (
        (k_pos[None, :] <= q_pos[:, None])
        & (k_seg[None, :] == q_seg[:, None])
        & (k_pos[None, :] >= 0)
    )

    q = queries.reshape(rows, heads_here, HD)
    scores = jnp.einsum("qhd,kd->hqk", q, k_win, preferred_element_type=jnp.float32) * scale
    masked = jnp.where(live[None], scores, jnp.float32(-1e30))
    peak = jnp.max(masked, axis=-1)
    expo = jnp.where(live[None], jnp.exp(masked - peak[..., None]), jnp.float32(0.0))
    denom = jnp.sum(expo, axis=-1)
    summed = jnp.einsum(
        "hqk,kd->hqd", expo.astype(jnp.bfloat16), v_win, preferred_element_type=jnp.float32
    )
    attn = summed / denom[..., None]
    attn_rows = jnp.transpose(attn, (1, 0, 2)).reshape(rows, heads_here * HD).astype(jnp.bfloat16)

    chunk = rows // n_seq
    total = relayout.shape[0]
    here = s * rows + jnp.arange(rows, dtype=jnp.int32)
    new_of = jnp.sum(
        jnp.where(relayout[None, :] == here[:, None], jnp.arange(total, dtype=jnp.int32)[None, :], 0),
        axis=1,
    )
    rank = jnp.sum((new_of[None, :] < new_of[:, None]).astype(jnp.int32), axis=1)
    send_sel = (rank[None, :] == jnp.arange(rows, dtype=jnp.int32)[:, None]).astype(jnp.bfloat16)
    to_send = jnp.dot(send_sel, attn_rows, preferred_element_type=jnp.float32).astype(jnp.bfloat16)
    arrived = lax.all_to_all(to_send, ("y", "x"), split_axis=0, concat_axis=0, tiled=True)

    src = lax.dynamic_slice_in_dim(relayout, s * rows, rows, 0) // rows
    before = jnp.arange(rows)[None, :] < jnp.arange(rows)[:, None]
    nth = jnp.sum((before & (src[None, :] == src[:, None])).astype(jnp.int32), axis=1)
    slot = src * chunk + nth
    per_dev = rows // (n_z * n_core)
    c = lax.axis_index("core")
    slot3 = slot.reshape(n_z, n_core, per_dev)
    cols = jnp.arange(rows, dtype=jnp.int32)[None, :]

    def project(which):
        chosen = jnp.take(slot3, which, axis=1).reshape(-1)
        sel = (chosen[:, None] == cols).astype(jnp.bfloat16)
        relaid = jnp.dot(sel, arrived, preferred_element_type=jnp.float32).astype(jnp.bfloat16)
        return jnp.dot(relaid, out_weight, preferred_element_type=jnp.float32).astype(jnp.bfloat16)

    part_other = project(n_core - 1 - c)
    got = lax.ppermute(part_other, "core", perm=[(0, 1), (1, 0)])
    part_own = project(c)
    half = (part_own.astype(jnp.float32) + got.astype(jnp.float32)).astype(jnp.bfloat16)
    return lax.psum_scatter(half, "z", scatter_dimension=0, tiled=True)

def solution(mesh):
    n_seq, n_tp = mesh.devices.shape
    n_x = 4
    mesh4 = Mesh(mesh.devices.reshape(n_seq // n_x, n_x, n_tp // 2, 2), ("y", "x", "z", "core"))
    seq = ("y", "x")
    tp = ("z", "core")
    return jax.shard_map(
        shards,
        mesh=mesh4,
        in_specs=(
            P(),
            P(),
            P(seq, tp),
            P(seq + tp, None),
            P(seq + tp, None),
            P(tp, None),
        ),
        out_specs=P(seq + tp, None),
        check_vma=False,
    )
```

```python
import jax
import jax.numpy as jnp
import numpy as np
from jax import lax
from jax.sharding import Mesh
from jax.sharding import PartitionSpec as P

QH = 32
KVH = 4
HD = 128
MOST_LEN = 2048


def shards(segment_ids, relayout, queries, keys, values, out_weight):
    rows = queries.shape[0]
    n_seq = lax.axis_size("y") * lax.axis_size("x")
    n_z = lax.axis_size("z")
    n_core = lax.axis_size("core")
    s = lax.axis_index("y") * lax.axis_size("x") + lax.axis_index("x")
    t = lax.axis_index("z") * n_core + lax.axis_index("core")
    heads_here = queries.shape[1] // HD
    group = QH // KVH
    kv_width = keys.shape[1]
    scale = HD ** (-0.5)
    back = -(-(MOST_LEN - 1) // rows)
    back = min(back, n_seq - 1)

    n_tp = n_z * n_core
    pieces = []
    for dest in range(n_tp):
        h = dest * heads_here // group
        pieces.append(jnp.concatenate([keys[:, h * HD:(h + 1) * HD], values[:, h * HD:(h + 1) * HD]], axis=1))
    own = lax.all_to_all(jnp.stack(pieces), ("z", "core"), split_axis=0, concat_axis=0, tiled=True)
    own = own.reshape(rows, 2 * HD)

    n_x = lax.axis_size("x")
    n_y = lax.axis_size("y")
    x = lax.axis_index("x")
    c = lax.axis_index("core")
    row = lax.all_gather(own, "x", axis=0, tiled=True)
    rows_back = -(-back // n_x)
    assert rows_back <= n_core
    perm = []
    for cc in range(n_core):
        k = cc + 1
        if k <= rows_back:
            perm += [(yy * n_core + cc, (yy + k) * n_core + cc) for yy in range(n_y - k)]
    fetched = lax.ppermute(row, ("y", "core"), perm=perm)
    swapped = lax.ppermute(fetched, "core", perm=[(i, (i + 1) % n_core) for i in range(n_core)])
    earlier = [jnp.where(c == k - 1, fetched, swapped) for k in range(rows_back, 0, -1)]
    kv_all = jnp.concatenate(earlier + [row], axis=0)
    n_keys = (back + 1) * rows
    first = (rows_back * n_x - back + x) * rows
    kv_win = lax.dynamic_slice_in_dim(kv_all, first, n_keys, 0)
    k_win = kv_win[:, :HD]
    v_win = kv_win[:, HD:]

    q_pos = s * rows + jnp.arange(rows, dtype=jnp.int32)
    k_pos = (s - back) * rows + jnp.arange(n_keys, dtype=jnp.int32)
    q_seg = lax.dynamic_slice_in_dim(segment_ids, s * rows, rows, 0)
    seg_pad = jnp.concatenate([jnp.full((back * rows,), -1, jnp.int32), segment_ids])
    k_seg = lax.dynamic_slice_in_dim(seg_pad, s * rows, n_keys, 0)
    live = (
        (k_pos[None, :] <= q_pos[:, None])
        & (k_seg[None, :] == q_seg[:, None])
        & (k_pos[None, :] >= 0)
    )

    q = queries.reshape(rows, heads_here, HD)
    scores = jnp.einsum("qhd,kd->hqk", q, k_win, preferred_element_type=jnp.float32) * scale
    masked = jnp.where(live[None], scores, jnp.float32(-1e30))
    peak = jnp.max(masked, axis=-1)
    expo = jnp.where(live[None], jnp.exp(masked - peak[..., None]), jnp.float32(0.0))
    denom = jnp.sum(expo, axis=-1)
    summed = jnp.einsum(
        "hqk,kd->hqd", expo.astype(jnp.bfloat16), v_win, preferred_element_type=jnp.float32
    )
    attn = summed / denom[..., None]
    attn_rows = jnp.transpose(attn, (1, 0, 2)).reshape(rows, heads_here * HD).astype(jnp.bfloat16)

    chunk = rows // n_seq
    total = relayout.shape[0]
    here = s * rows + jnp.arange(rows, dtype=jnp.int32)
    new_of = jnp.sum(
        jnp.where(relayout[None, :] == here[:, None], jnp.arange(total, dtype=jnp.int32)[None, :], 0),
        axis=1,
    )
    rank = jnp.sum((new_of[None, :] < new_of[:, None]).astype(jnp.int32), axis=1)
    send_sel = (rank[None, :] == jnp.arange(rows, dtype=jnp.int32)[:, None]).astype(jnp.bfloat16)
    to_send = jnp.dot(send_sel, attn_rows, preferred_element_type=jnp.float32).astype(jnp.bfloat16)
    arrived = lax.all_to_all(to_send, ("y", "x"), split_axis=0, concat_axis=0, tiled=True)

    src = lax.dynamic_slice_in_dim(relayout, s * rows, rows, 0) // rows
    before = jnp.arange(rows)[None, :] < jnp.arange(rows)[:, None]
    nth = jnp.sum((before & (src[None, :] == src[:, None])).astype(jnp.int32), axis=1)
    slot = src * chunk + nth
    per_dev = rows // (n_z * n_core)
    slot3 = slot.reshape(n_z, n_core, per_dev)
    cols = jnp.arange(rows, dtype=jnp.int32)[None, :]

    def project(which):
        chosen = jnp.take(slot3, which, axis=1).reshape(-1)
        sel = (chosen[:, None] == cols).astype(jnp.bfloat16)
        relaid = jnp.dot(sel, arrived, preferred_element_type=jnp.float32).astype(jnp.bfloat16)
        return jnp.dot(relaid, out_weight, preferred_element_type=jnp.float32).astype(jnp.bfloat16)

    part_other = project(n_core - 1 - c)
    got = lax.ppermute(part_other, "core", perm=[(0, 1), (1, 0)])
    part_own = project(c)
    half = (part_own.astype(jnp.float32) + got.astype(jnp.float32)).astype(jnp.bfloat16)
    return lax.psum_scatter(half, "z", scatter_dimension=0, tiled=True)

def solution(mesh):
    n_seq, n_tp = mesh.devices.shape
    n_x = 4
    mesh4 = Mesh(mesh.devices.reshape(n_seq // n_x, n_x, n_tp // 2, 2), ("y", "x", "z", "core"))
    seq = ("y", "x")
    tp = ("z", "core")
    return jax.shard_map(
        shards,
        mesh=mesh4,
        in_specs=(
            P(),
            P(),
            P(seq, tp),
            P(seq + tp, None),
            P(seq + tp, None),
            P(tp, None),
        ),
        out_specs=P(seq + tp, None),
        check_vma=False,
    )
```

```python
import jax
import jax.numpy as jnp
import numpy as np
from jax import lax
from jax.sharding import Mesh
from jax.sharding import PartitionSpec as P

QH = 32
KVH = 4
HD = 128
MOST_LEN = 2048


def shards(segment_ids, relayout, queries, keys, values, out_weight):
    rows = queries.shape[0]
    n_seq = lax.axis_size("y") * lax.axis_size("x")
    n_z = lax.axis_size("z")
    n_core = lax.axis_size("core")
    s = lax.axis_index("y") * lax.axis_size("x") + lax.axis_index("x")
    t = lax.axis_index("z") * n_core + lax.axis_index("core")
    heads_here = queries.shape[1] // HD
    group = QH // KVH
    kv_width = keys.shape[1]
    scale = HD ** (-0.5)
    back = -(-(MOST_LEN - 1) // rows)
    back = min(back, n_seq - 1)

    n_tp = n_z * n_core
    kv_heads = kv_width // HD
    heads_of = np.arange(n_tp) * heads_here // group
    k_h = jnp.transpose(keys.reshape(keys.shape[0], kv_heads, HD), (1, 0, 2))
    v_h = jnp.transpose(values.reshape(values.shape[0], kv_heads, HD), (1, 0, 2))
    pieces = jnp.concatenate([k_h, v_h], axis=2)[heads_of]
    own = lax.all_to_all(pieces, ("z", "core"), split_axis=0, concat_axis=0, tiled=True)
    own = own.reshape(rows, 2 * HD)

    n_x = lax.axis_size("x")
    n_y = lax.axis_size("y")
    x = lax.axis_index("x")
    c = lax.axis_index("core")
    row = lax.all_to_all(jnp.broadcast_to(own[None], (n_x,) + own.shape), "x", split_axis=0, concat_axis=0, tiled=True)
    row = row.reshape(n_x * rows, own.shape[1])
    rows_back = -(-back // n_x)
    assert rows_back <= n_core
    perm = []
    for cc in range(n_core):
        k = cc + 1
        if k <= rows_back:
            perm += [(yy * n_core + cc, (yy + k) * n_core + cc) for yy in range(n_y - k)]
    fetched = lax.ppermute(row, ("y", "core"), perm=perm)
    swapped = lax.ppermute(fetched, "core", perm=[(i, (i + 1) % n_core) for i in range(n_core)])
    earlier = [jnp.where(c == k - 1, fetched, swapped) for k in range(rows_back, 0, -1)]
    kv_all = jnp.concatenate(earlier + [row], axis=0)
    n_keys = (back + 1) * rows
    first = (rows_back * n_x - back + x) * rows
    kv_win = lax.dynamic_slice_in_dim(kv_all, first, n_keys, 0)
    k_win = kv_win[:, :HD]
    v_win = kv_win[:, HD:]

    q_pos = s * rows + jnp.arange(rows, dtype=jnp.int32)
    k_pos = (s - back) * rows + jnp.arange(n_keys, dtype=jnp.int32)
    q_seg = lax.dynamic_slice_in_dim(segment_ids, s * rows, rows, 0)
    seg_pad = jnp.concatenate([jnp.full((back * rows,), -1, jnp.int32), segment_ids])
    k_seg = lax.dynamic_slice_in_dim(seg_pad, s * rows, n_keys, 0)
    live = (
        (k_pos[None, :] <= q_pos[:, None])
        & (k_seg[None, :] == q_seg[:, None])
        & (k_pos[None, :] >= 0)
    )

    q = queries.reshape(rows, heads_here, HD)
    scores = jnp.einsum("qhd,kd->hqk", q, k_win, preferred_element_type=jnp.float32) * scale
    masked = jnp.where(live[None], scores, jnp.float32(-1e30))
    peak = jnp.max(masked, axis=-1)
    expo = jnp.where(live[None], jnp.exp(masked - peak[..., None]), jnp.float32(0.0))
    denom = jnp.sum(expo, axis=-1)
    summed = jnp.einsum(
        "hqk,kd->hqd", expo.astype(jnp.bfloat16), v_win, preferred_element_type=jnp.float32
    )
    attn = summed / denom[..., None]
    attn_rows = jnp.transpose(attn, (1, 0, 2)).reshape(rows, heads_here * HD).astype(jnp.bfloat16)

    chunk = rows // n_seq
    total = relayout.shape[0]
    here = s * rows + jnp.arange(rows, dtype=jnp.int32)
    new_of = jnp.sum(
        jnp.where(relayout[None, :] == here[:, None], jnp.arange(total, dtype=jnp.int32)[None, :], 0),
        axis=1,
    )
    rank = jnp.sum((new_of[None, :] < new_of[:, None]).astype(jnp.int32), axis=1)
    send_sel = (rank[None, :] == jnp.arange(rows, dtype=jnp.int32)[:, None]).astype(jnp.bfloat16)
    to_send = jnp.dot(send_sel, attn_rows, preferred_element_type=jnp.float32).astype(jnp.bfloat16)
    arrived = lax.all_to_all(to_send, ("y", "x"), split_axis=0, concat_axis=0, tiled=True)

    src = lax.dynamic_slice_in_dim(relayout, s * rows, rows, 0) // rows
    before = jnp.arange(rows)[None, :] < jnp.arange(rows)[:, None]
    nth = jnp.sum((before & (src[None, :] == src[:, None])).astype(jnp.int32), axis=1)
    slot = src * chunk + nth
    per_dev = rows // (n_z * n_core)
    slot3 = slot.reshape(n_z, n_core, per_dev)
    cols = jnp.arange(rows, dtype=jnp.int32)[None, :]

    def project(which):
        chosen = jnp.take(slot3, which, axis=1).reshape(-1)
        sel = (chosen[:, None] == cols).astype(jnp.bfloat16)
        relaid = jnp.dot(sel, arrived, preferred_element_type=jnp.float32).astype(jnp.bfloat16)
        return jnp.dot(relaid, out_weight, preferred_element_type=jnp.float32).astype(jnp.bfloat16)

    part_other = project(n_core - 1 - c)
    got = lax.ppermute(part_other, "core", perm=[(0, 1), (1, 0)])
    part_own = project(c)
    half = (part_own.astype(jnp.float32) + got.astype(jnp.float32)).astype(jnp.bfloat16)
    ring_cols = 3072
    sc_cols = half.shape[1] - ring_cols
    from_sc = lax.psum_scatter(half[:, :sc_cols], "z", scatter_dimension=0, tiled=True)
    z = lax.axis_index("z")
    step = 1 - 2 * c
    chunks = half[:, sc_cols:].reshape(n_z, per_dev, ring_cols)
    ring_perm = []
    for zz in range(n_z):
        ring_perm.append((zz * n_core, ((zz + 1) % n_z) * n_core))
        ring_perm.append((zz * n_core + 1, ((zz - 1) % n_z) * n_core + 1))

    def own_chunk(k):
        return lax.dynamic_index_in_dim(chunks, (z - step * k) % n_z, 0, keepdims=False)

    acc = own_chunk(1)
    for k in range(1, n_z):
        got_k = lax.ppermute(acc, ("z", "core"), perm=ring_perm)
        acc = (got_k.astype(jnp.float32) + own_chunk(k + 1).astype(jnp.float32)).astype(jnp.bfloat16)
    return jnp.concatenate([from_sc, acc], axis=1)

def solution(mesh):
    n_seq, n_tp = mesh.devices.shape
    n_x = 4
    mesh4 = Mesh(mesh.devices.reshape(n_seq // n_x, n_x, n_tp // 2, 2), ("y", "x", "z", "core"))
    seq = ("y", "x")
    tp = ("z", "core")
    return jax.shard_map(
        shards,
        mesh=mesh4,
        in_specs=(
            P(),
            P(),
            P(seq, tp),
            P(seq + tp, None),
            P(seq + tp, None),
            P(tp, None),
        ),
        out_specs=P(seq + tp, None),
        check_vma=False,
    )
```

```python
import jax
import jax.numpy as jnp
import numpy as np
from jax import lax
from jax.sharding import Mesh
from jax.sharding import PartitionSpec as P

QH = 32
KVH = 4
HD = 128
MOST_LEN = 2048


def shards(segment_ids, relayout, queries, keys, values, out_weight):
    rows = queries.shape[0]
    n_seq = lax.axis_size("y") * lax.axis_size("x")
    n_z = lax.axis_size("z")
    n_core = lax.axis_size("core")
    s = lax.axis_index("y") * lax.axis_size("x") + lax.axis_index("x")
    t = lax.axis_index("z") * n_core + lax.axis_index("core")
    heads_here = queries.shape[1] // HD
    group = QH // KVH
    kv_width = keys.shape[1]
    scale = HD ** (-0.5)
    back = -(-(MOST_LEN - 1) // rows)
    back = min(back, n_seq - 1)

    n_tp = n_z * n_core
    kv_heads = kv_width // HD
    n_x = lax.axis_size("x")
    heads_of = np.tile(np.arange(n_tp) * heads_here // group, n_x)
    k_h = jnp.transpose(keys.reshape(keys.shape[0], kv_heads, HD), (1, 0, 2))
    v_h = jnp.transpose(values.reshape(values.shape[0], kv_heads, HD), (1, 0, 2))
    pieces = jnp.concatenate([k_h, v_h], axis=2)[heads_of]
    row = lax.all_to_all(pieces, ("x", "z", "core"), split_axis=0, concat_axis=0, tiled=True)
    row = row.reshape(n_x * rows, 2 * HD)

    n_y = lax.axis_size("y")
    x = lax.axis_index("x")
    c = lax.axis_index("core")
    rows_back = -(-back // n_x)
    assert rows_back <= n_core
    perm = []
    for cc in range(n_core):
        k = cc + 1
        if k <= rows_back:
            perm += [(yy * n_core + cc, (yy + k) * n_core + cc) for yy in range(n_y - k)]
    fetched = lax.ppermute(row, ("y", "core"), perm=perm)
    swapped = lax.ppermute(fetched, "core", perm=[(i, (i + 1) % n_core) for i in range(n_core)])
    earlier = [jnp.where(c == k - 1, fetched, swapped) for k in range(rows_back, 0, -1)]
    kv_all = jnp.concatenate(earlier + [row], axis=0)
    n_keys = (back + 1) * rows
    first = (rows_back * n_x - back + x) * rows
    kv_win = lax.dynamic_slice_in_dim(kv_all, first, n_keys, 0)
    k_win = kv_win[:, :HD]
    v_win = kv_win[:, HD:]

    q_pos = s * rows + jnp.arange(rows, dtype=jnp.int32)
    k_pos = (s - back) * rows + jnp.arange(n_keys, dtype=jnp.int32)
    q_seg = lax.dynamic_slice_in_dim(segment_ids, s * rows, rows, 0)
    seg_pad = jnp.concatenate([jnp.full((back * rows,), -1, jnp.int32), segment_ids])
    k_seg = lax.dynamic_slice_in_dim(seg_pad, s * rows, n_keys, 0)
    live = (
        (k_pos[None, :] <= q_pos[:, None])
        & (k_seg[None, :] == q_seg[:, None])
        & (k_pos[None, :] >= 0)
    )

    q = queries.reshape(rows, heads_here, HD)
    scores = jnp.einsum("qhd,kd->hqk", q, k_win, preferred_element_type=jnp.float32) * scale
    masked = jnp.where(live[None], scores, jnp.float32(-1e30))
    peak = jnp.max(masked, axis=-1)
    expo = jnp.where(live[None], jnp.exp(masked - peak[..., None]), jnp.float32(0.0))
    denom = jnp.sum(expo, axis=-1)
    summed = jnp.einsum(
        "hqk,kd->hqd", expo.astype(jnp.bfloat16), v_win, preferred_element_type=jnp.float32
    )
    attn = summed / denom[..., None]
    attn_rows = jnp.transpose(attn, (1, 0, 2)).reshape(rows, heads_here * HD).astype(jnp.bfloat16)

    chunk = rows // n_seq
    total = relayout.shape[0]
    here = s * rows + jnp.arange(rows, dtype=jnp.int32)
    new_of = jnp.sum(
        jnp.where(relayout[None, :] == here[:, None], jnp.arange(total, dtype=jnp.int32)[None, :], 0),
        axis=1,
    )
    rank = jnp.sum((new_of[None, :] < new_of[:, None]).astype(jnp.int32), axis=1)
    send_sel = (rank[None, :] == jnp.arange(rows, dtype=jnp.int32)[:, None]).astype(jnp.bfloat16)
    to_send = jnp.dot(send_sel, attn_rows, preferred_element_type=jnp.float32).astype(jnp.bfloat16)
    arrived = lax.all_to_all(to_send, ("y", "x"), split_axis=0, concat_axis=0, tiled=True)

    src = lax.dynamic_slice_in_dim(relayout, s * rows, rows, 0) // rows
    before = jnp.arange(rows)[None, :] < jnp.arange(rows)[:, None]
    nth = jnp.sum((before & (src[None, :] == src[:, None])).astype(jnp.int32), axis=1)
    slot = src * chunk + nth
    per_dev = rows // (n_z * n_core)
    slot3 = slot.reshape(n_z, n_core, per_dev)
    cols = jnp.arange(rows, dtype=jnp.int32)[None, :]

    def project(which):
        chosen = jnp.take(slot3, which, axis=1).reshape(-1)
        sel = (chosen[:, None] == cols).astype(jnp.bfloat16)
        relaid = jnp.dot(sel, arrived, preferred_element_type=jnp.float32).astype(jnp.bfloat16)
        return jnp.dot(relaid, out_weight, preferred_element_type=jnp.float32).astype(jnp.bfloat16)

    part_other = project(n_core - 1 - c)
    got = lax.ppermute(part_other, "core", perm=[(0, 1), (1, 0)])
    part_own = project(c)
    half = (part_own.astype(jnp.float32) + got.astype(jnp.float32)).astype(jnp.bfloat16)
    return lax.psum_scatter(half, "z", scatter_dimension=0, tiled=True)

def solution(mesh):
    n_seq, n_tp = mesh.devices.shape
    n_x = 4
    mesh4 = Mesh(mesh.devices.reshape(n_seq // n_x, n_x, n_tp // 2, 2), ("y", "x", "z", "core"))
    seq = ("y", "x")
    tp = ("z", "core")
    return jax.shard_map(
        shards,
        mesh=mesh4,
        in_specs=(
            P(),
            P(),
            P(seq, tp),
            P(seq + tp, None),
            P(seq + tp, None),
            P(tp, None),
        ),
        out_specs=P(seq + tp, None),
        check_vma=False,
    )
```

```python
import jax
import jax.numpy as jnp
import numpy as np
from jax import lax
from jax.sharding import Mesh
from jax.sharding import PartitionSpec as P

QH = 32
KVH = 4
HD = 128
MOST_LEN = 2048


def shards(segment_ids, relayout, queries, keys, values, out_weight):
    rows = queries.shape[0]
    n_seq = lax.axis_size("y") * lax.axis_size("x")
    n_zh = lax.axis_size("zh")
    n_zl = lax.axis_size("zl")
    n_z = n_zh * n_zl
    n_core = lax.axis_size("core")
    s = lax.axis_index("y") * lax.axis_size("x") + lax.axis_index("x")
    t = (lax.axis_index("zh") * n_zl + lax.axis_index("zl")) * n_core + lax.axis_index("core")
    heads_here = queries.shape[1] // HD
    group = QH // KVH
    kv_width = keys.shape[1]
    scale = HD ** (-0.5)
    back = -(-(MOST_LEN - 1) // rows)
    back = min(back, n_seq - 1)

    n_tp = n_z * n_core
    kv_heads = kv_width // HD
    n_x = lax.axis_size("x")
    heads_of = np.tile(np.arange(n_tp) * heads_here // group, n_x)
    k_h = jnp.transpose(keys.reshape(keys.shape[0], kv_heads, HD), (1, 0, 2))
    v_h = jnp.transpose(values.reshape(values.shape[0], kv_heads, HD), (1, 0, 2))
    pieces = jnp.concatenate([k_h, v_h], axis=2)[heads_of]
    row = lax.all_to_all(pieces, ("x", "zh", "zl", "core"), split_axis=0, concat_axis=0, tiled=True)
    row = row.reshape(n_x * rows, 2 * HD)

    n_y = lax.axis_size("y")
    x = lax.axis_index("x")
    c = lax.axis_index("core")
    rows_back = -(-back // n_x)
    assert rows_back <= n_core
    perm = []
    for cc in range(n_core):
        k = cc + 1
        if k <= rows_back:
            perm += [(yy * n_core + cc, (yy + k) * n_core + cc) for yy in range(n_y - k)]
    fetched = lax.ppermute(row, ("y", "core"), perm=perm)
    swapped = lax.ppermute(fetched, "core", perm=[(i, (i + 1) % n_core) for i in range(n_core)])
    earlier = [jnp.where(c == k - 1, fetched, swapped) for k in range(rows_back, 0, -1)]
    kv_all = jnp.concatenate(earlier + [row], axis=0)
    n_keys = (back + 1) * rows
    first = (rows_back * n_x - back + x) * rows
    kv_win = lax.dynamic_slice_in_dim(kv_all, first, n_keys, 0)
    k_win = kv_win[:, :HD]
    v_win = kv_win[:, HD:]

    q_pos = s * rows + jnp.arange(rows, dtype=jnp.int32)
    k_pos = (s - back) * rows + jnp.arange(n_keys, dtype=jnp.int32)
    q_seg = lax.dynamic_slice_in_dim(segment_ids, s * rows, rows, 0)
    seg_pad = jnp.concatenate([jnp.full((back * rows,), -1, jnp.int32), segment_ids])
    k_seg = lax.dynamic_slice_in_dim(seg_pad, s * rows, n_keys, 0)
    live = (
        (k_pos[None, :] <= q_pos[:, None])
        & (k_seg[None, :] == q_seg[:, None])
        & (k_pos[None, :] >= 0)
    )

    q = queries.reshape(rows, heads_here, HD)
    scores = jnp.einsum("qhd,kd->hqk", q, k_win, preferred_element_type=jnp.float32) * scale
    masked = jnp.where(live[None], scores, jnp.float32(-1e30))
    peak = jnp.max(masked, axis=-1)
    expo = jnp.where(live[None], jnp.exp(masked - peak[..., None]), jnp.float32(0.0))
    denom = jnp.sum(expo, axis=-1)
    summed = jnp.einsum(
        "hqk,kd->hqd", expo.astype(jnp.bfloat16), v_win, preferred_element_type=jnp.float32
    )
    attn = summed / denom[..., None]
    attn_rows = jnp.transpose(attn, (1, 0, 2)).reshape(rows, heads_here * HD).astype(jnp.bfloat16)

    chunk = rows // n_seq
    total = relayout.shape[0]
    here = s * rows + jnp.arange(rows, dtype=jnp.int32)
    new_of = jnp.sum(
        jnp.where(relayout[None, :] == here[:, None], jnp.arange(total, dtype=jnp.int32)[None, :], 0),
        axis=1,
    )
    rank = jnp.sum((new_of[None, :] < new_of[:, None]).astype(jnp.int32), axis=1)
    send_sel = (rank[None, :] == jnp.arange(rows, dtype=jnp.int32)[:, None]).astype(jnp.bfloat16)
    to_send = jnp.dot(send_sel, attn_rows, preferred_element_type=jnp.float32).astype(jnp.bfloat16)
    arrived = lax.all_to_all(to_send, ("y", "x"), split_axis=0, concat_axis=0, tiled=True)

    src = lax.dynamic_slice_in_dim(relayout, s * rows, rows, 0) // rows
    before = jnp.arange(rows)[None, :] < jnp.arange(rows)[:, None]
    nth = jnp.sum((before & (src[None, :] == src[:, None])).astype(jnp.int32), axis=1)
    slot = src * chunk + nth
    per_dev = rows // (n_z * n_core)
    slot3 = jnp.transpose(slot.reshape(n_zh, n_zl, n_core, per_dev), (1, 0, 2, 3)).reshape(n_z, n_core, per_dev)
    cols = jnp.arange(rows, dtype=jnp.int32)[None, :]

    def project(which):
        chosen = jnp.take(slot3, which, axis=1).reshape(-1)
        sel = (chosen[:, None] == cols).astype(jnp.bfloat16)
        relaid = jnp.dot(sel, arrived, preferred_element_type=jnp.float32).astype(jnp.bfloat16)
        return jnp.dot(relaid, out_weight, preferred_element_type=jnp.float32).astype(jnp.bfloat16)

    part_other = project(n_core - 1 - c)
    got = lax.ppermute(part_other, "core", perm=[(0, 1), (1, 0)])
    part_own = lax.optimization_barrier(project(c))
    half = (part_own.astype(jnp.float32) + got.astype(jnp.float32)).astype(jnp.bfloat16)
    quarter = lax.psum_scatter(half, "zl", scatter_dimension=0, tiled=True)
    return lax.psum_scatter(quarter, "zh", scatter_dimension=0, tiled=True)

def solution(mesh):
    n_seq, n_tp = mesh.devices.shape
    n_x = 4
    n_zl = 4
    shape = (n_seq // n_x, n_x, n_tp // (2 * n_zl), n_zl, 2)
    mesh5 = Mesh(mesh.devices.reshape(shape), ("y", "x", "zh", "zl", "core"))
    seq = ("y", "x")
    tp = ("zh", "zl", "core")
    return jax.shard_map(
        shards,
        mesh=mesh5,
        in_specs=(
            P(),
            P(),
            P(seq, tp),
            P(seq + tp, None),
            P(seq + tp, None),
            P(tp, None),
        ),
        out_specs=P(seq + tp, None),
        check_vma=False,
    )
```

```python
import jax
import jax.numpy as jnp
import numpy as np
from jax import lax
from jax.sharding import Mesh
from jax.sharding import PartitionSpec as P

QH = 32
KVH = 4
HD = 128
MOST_LEN = 2048


def shards(segment_ids, relayout, queries, keys, values, out_weight):
    rows = queries.shape[0]
    n_seq = lax.axis_size("y") * lax.axis_size("x")
    n_z = lax.axis_size("z")
    n_core = lax.axis_size("core")
    s = lax.axis_index("y") * lax.axis_size("x") + lax.axis_index("x")
    t = lax.axis_index("z") * n_core + lax.axis_index("core")
    heads_here = queries.shape[1] // HD
    group = QH // KVH
    kv_width = keys.shape[1]
    scale = HD ** (-0.5)
    back = -(-(MOST_LEN - 1) // rows)
    back = min(back, n_seq - 1)

    n_tp = n_z * n_core
    kv_heads = kv_width // HD
    n_x = lax.axis_size("x")
    heads_of = np.tile(np.arange(n_tp) * heads_here // group, n_x)
    k_h = jnp.transpose(keys.reshape(keys.shape[0], kv_heads, HD), (1, 0, 2))
    v_h = jnp.transpose(values.reshape(values.shape[0], kv_heads, HD), (1, 0, 2))
    pieces = jnp.concatenate([k_h, v_h], axis=2)[heads_of]
    row = lax.all_to_all(pieces, ("x", "z", "core"), split_axis=0, concat_axis=0, tiled=True)
    row = row.reshape(n_x * rows, 2 * HD)

    n_y = lax.axis_size("y")
    x = lax.axis_index("x")
    c = lax.axis_index("core")
    rows_back = -(-back // n_x)
    assert rows_back <= n_core
    perm = []
    for cc in range(n_core):
        k = cc + 1
        if k <= rows_back:
            perm += [(yy * n_core + cc, (yy + k) * n_core + cc) for yy in range(n_y - k)]
    fetched = lax.ppermute(row, ("y", "core"), perm=perm)
    swapped = lax.ppermute(fetched, "core", perm=[(i, (i + 1) % n_core) for i in range(n_core)])
    earlier = [jnp.where(c == k - 1, fetched, swapped) for k in range(rows_back, 0, -1)]
    kv_all = jnp.concatenate(earlier + [row], axis=0)
    n_keys = (back + 1) * rows
    first = (rows_back * n_x - back + x) * rows
    kv_win = lax.dynamic_slice_in_dim(kv_all, first, n_keys, 0)
    k_win = kv_win[:, :HD]
    v_win = kv_win[:, HD:]

    q_pos = s * rows + jnp.arange(rows, dtype=jnp.int32)
    k_pos = (s - back) * rows + jnp.arange(n_keys, dtype=jnp.int32)
    q_seg = lax.dynamic_slice_in_dim(segment_ids, s * rows, rows, 0)
    seg_pad = jnp.concatenate([jnp.full((back * rows,), -1, jnp.int32), segment_ids])
    k_seg = lax.dynamic_slice_in_dim(seg_pad, s * rows, n_keys, 0)
    live = (
        (k_pos[None, :] <= q_pos[:, None])
        & (k_seg[None, :] == q_seg[:, None])
        & (k_pos[None, :] >= 0)
    )

    q = queries.reshape(rows, heads_here, HD)
    scores = jnp.einsum("qhd,kd->hqk", q, k_win, preferred_element_type=jnp.float32) * scale
    masked = jnp.where(live[None], scores, jnp.float32(-1e30))
    peak = jnp.max(masked, axis=-1)
    expo = jnp.where(live[None], jnp.exp(masked - peak[..., None]), jnp.float32(0.0))
    denom = jnp.sum(expo, axis=-1)
    summed = jnp.einsum(
        "hqk,kd->hqd", expo.astype(jnp.bfloat16), v_win, preferred_element_type=jnp.float32
    )
    attn = summed / denom[..., None]
    attn_rows = jnp.transpose(attn, (1, 0, 2)).reshape(rows, heads_here * HD).astype(jnp.bfloat16)

    chunk = rows // n_seq
    total = relayout.shape[0]
    here = s * rows + jnp.arange(rows, dtype=jnp.int32)
    new_of = jnp.sum(
        jnp.where(relayout[None, :] == here[:, None], jnp.arange(total, dtype=jnp.int32)[None, :], 0),
        axis=1,
    )
    rank = jnp.sum((new_of[None, :] < new_of[:, None]).astype(jnp.int32), axis=1)
    send_sel = (rank[None, :] == jnp.arange(rows, dtype=jnp.int32)[:, None]).astype(jnp.bfloat16)
    to_send = jnp.dot(send_sel, attn_rows, preferred_element_type=jnp.float32).astype(jnp.bfloat16)
    arrived = lax.all_to_all(to_send, ("y", "x"), split_axis=0, concat_axis=0, tiled=True)

    src = lax.dynamic_slice_in_dim(relayout, s * rows, rows, 0) // rows
    before = jnp.arange(rows)[None, :] < jnp.arange(rows)[:, None]
    nth = jnp.sum((before & (src[None, :] == src[:, None])).astype(jnp.int32), axis=1)
    slot = src * chunk + nth
    per_dev = rows // (n_z * n_core)
    slot3 = slot.reshape(n_z, n_core, per_dev)
    cols = jnp.arange(rows, dtype=jnp.int32)[None, :]

    def project(which):
        chosen = jnp.take(slot3, which, axis=1).reshape(-1)
        sel = (chosen[:, None] == cols).astype(jnp.bfloat16)
        relaid = jnp.dot(sel, arrived, preferred_element_type=jnp.float32).astype(jnp.bfloat16)
        return jnp.dot(relaid, out_weight, preferred_element_type=jnp.float32).astype(jnp.bfloat16)

    part_other = project(n_core - 1 - c)
    got = lax.ppermute(part_other, "core", perm=[(0, 1), (1, 0)])
    part_own = lax.optimization_barrier(project(c))
    half = (part_own.astype(jnp.float32) + got.astype(jnp.float32)).astype(jnp.bfloat16)
    return lax.psum_scatter(half, "z", scatter_dimension=0, tiled=True)

def solution(mesh):
    n_seq, n_tp = mesh.devices.shape
    n_x = 4
    mesh4 = Mesh(mesh.devices.reshape(n_seq // n_x, n_x, n_tp // 2, 2), ("y", "x", "z", "core"))
    seq = ("y", "x")
    tp = ("z", "core")
    return jax.shard_map(
        shards,
        mesh=mesh4,
        in_specs=(
            P(),
            P(),
            P(seq, tp),
            P(seq + tp, None),
            P(seq + tp, None),
            P(tp, None),
        ),
        out_specs=P(seq + tp, None),
        check_vma=False,
    )
```

```python
import functools

import jax
import jax.numpy as jnp
import numpy as np
from jax import lax
from jax.experimental import pallas as pl
from jax.sharding import Mesh
from jax.sharding import PartitionSpec as P

QH = 32
KVH = 4
HD = 128
MOST_LEN = 2048


def _attention_body(scale, q_ref, k_ref, v_ref, qp_ref, qs_ref, kp_ref, ks_ref, o_ref):
    s = lax.dot_general(
        q_ref[...], k_ref[...], (((1,), (1,)), ((), ())), preferred_element_type=jnp.float32
    ) * scale
    live = (kp_ref[...] <= qp_ref[...]) & (ks_ref[...] == qs_ref[...])
    masked = jnp.where(live, s, jnp.float32(-1e30))
    peak = jnp.max(masked, axis=1, keepdims=True)
    expo = jnp.where(live, jnp.exp(masked - peak), jnp.float32(0.0))
    denom = jnp.sum(expo, axis=1, keepdims=True)
    summed = jnp.dot(expo.astype(jnp.bfloat16), v_ref[...], preferred_element_type=jnp.float32)
    o_ref[...] = (summed / denom).astype(o_ref.dtype)


def attention(q, kv, q_pos, q_seg, k_pos, k_seg, scale):
    rows, width = q.shape
    heads = width // HD
    n_keys = kv.shape[0]
    return pl.pallas_call(
        functools.partial(_attention_body, scale),
        grid=(heads,),
        in_specs=[
            pl.BlockSpec((rows, HD), lambda h: (0, h)),
            pl.BlockSpec((n_keys, HD), lambda h: (0, 0)),
            pl.BlockSpec((n_keys, HD), lambda h: (0, 1)),
            pl.BlockSpec((rows, 1), lambda h: (0, 0)),
            pl.BlockSpec((rows, 1), lambda h: (0, 0)),
            pl.BlockSpec((1, n_keys), lambda h: (0, 0)),
            pl.BlockSpec((1, n_keys), lambda h: (0, 0)),
        ],
        out_specs=pl.BlockSpec((rows, HD), lambda h: (0, h)),
        out_shape=jax.ShapeDtypeStruct((rows, width), jnp.bfloat16),
        cost_estimate=pl.CostEstimate(
            flops=4 * rows * n_keys * HD * heads,
            transcendentals=rows * n_keys * heads,
            bytes_accessed=2 * (2 * rows * width + 2 * n_keys * HD),
        ),
    )(
        q,
        kv,
        kv,
        q_pos.reshape(rows, 1),
        q_seg.reshape(rows, 1),
        k_pos.reshape(1, n_keys),
        k_seg.reshape(1, n_keys),
    )


def shards(segment_ids, relayout, queries, keys, values, out_weight):
    rows = queries.shape[0]
    n_seq = lax.axis_size("y") * lax.axis_size("x")
    n_z = lax.axis_size("z")
    n_core = lax.axis_size("core")
    s = lax.axis_index("y") * lax.axis_size("x") + lax.axis_index("x")
    t = lax.axis_index("z") * n_core + lax.axis_index("core")
    heads_here = queries.shape[1] // HD
    group = QH // KVH
    kv_width = keys.shape[1]
    scale = HD ** (-0.5)
    back = -(-(MOST_LEN - 1) // rows)
    back = min(back, n_seq - 1)

    n_tp = n_z * n_core
    kv_heads = kv_width // HD
    n_x = lax.axis_size("x")
    heads_of = np.tile(np.arange(n_tp) * heads_here // group, n_x)
    k_h = jnp.transpose(keys.reshape(keys.shape[0], kv_heads, HD), (1, 0, 2))
    v_h = jnp.transpose(values.reshape(values.shape[0], kv_heads, HD), (1, 0, 2))
    pieces = jnp.concatenate([k_h, v_h], axis=2)[heads_of]
    row = lax.all_to_all(pieces, ("x", "z", "core"), split_axis=0, concat_axis=0, tiled=True)
    row = row.reshape(n_x * rows, 2 * HD)

    n_y = lax.axis_size("y")
    x = lax.axis_index("x")
    c = lax.axis_index("core")
    rows_back = -(-back // n_x)
    assert rows_back <= n_core
    perm = []
    for cc in range(n_core):
        k = cc + 1
        if k <= rows_back:
            perm += [(yy * n_core + cc, (yy + k) * n_core + cc) for yy in range(n_y - k)]
    fetched = lax.ppermute(row, ("y", "core"), perm=perm)
    swapped = lax.ppermute(fetched, "core", perm=[(i, (i + 1) % n_core) for i in range(n_core)])
    earlier = [jnp.where(c == k - 1, fetched, swapped) for k in range(rows_back, 0, -1)]
    kv_all = jnp.concatenate(earlier + [row], axis=0)
    n_keys = (back + 1) * rows
    first = (rows_back * n_x - back + x) * rows
    kv_win = lax.dynamic_slice_in_dim(kv_all, first, n_keys, 0)

    q_pos = s * rows + jnp.arange(rows, dtype=jnp.int32)
    k_pos = (s - back) * rows + jnp.arange(n_keys, dtype=jnp.int32)
    q_seg = lax.dynamic_slice_in_dim(segment_ids, s * rows, rows, 0)
    seg_pad = jnp.concatenate([jnp.full((back * rows,), -1, jnp.int32), segment_ids])
    k_seg = lax.dynamic_slice_in_dim(seg_pad, s * rows, n_keys, 0)
    attn_rows = attention(queries, kv_win, q_pos, q_seg, k_pos, k_seg, scale)

    chunk = rows // n_seq
    total = relayout.shape[0]
    here = s * rows + jnp.arange(rows, dtype=jnp.int32)
    new_of = jnp.sum(
        jnp.where(relayout[None, :] == here[:, None], jnp.arange(total, dtype=jnp.int32)[None, :], 0),
        axis=1,
    )
    rank = jnp.sum((new_of[None, :] < new_of[:, None]).astype(jnp.int32), axis=1)
    send_sel = (rank[None, :] == jnp.arange(rows, dtype=jnp.int32)[:, None]).astype(jnp.bfloat16)
    to_send = jnp.dot(send_sel, attn_rows, preferred_element_type=jnp.float32).astype(jnp.bfloat16)
    arrived = lax.all_to_all(to_send, ("y", "x"), split_axis=0, concat_axis=0, tiled=True)

    src = lax.dynamic_slice_in_dim(relayout, s * rows, rows, 0) // rows
    before = jnp.arange(rows)[None, :] < jnp.arange(rows)[:, None]
    nth = jnp.sum((before & (src[None, :] == src[:, None])).astype(jnp.int32), axis=1)
    slot = src * chunk + nth
    per_dev = rows // (n_z * n_core)
    slot3 = slot.reshape(n_z, n_core, per_dev)
    cols = jnp.arange(rows, dtype=jnp.int32)[None, :]

    def project(which):
        chosen = jnp.take(slot3, which, axis=1).reshape(-1)
        sel = (chosen[:, None] == cols).astype(jnp.bfloat16)
        relaid = jnp.dot(sel, arrived, preferred_element_type=jnp.float32).astype(jnp.bfloat16)
        return jnp.dot(relaid, out_weight, preferred_element_type=jnp.float32).astype(jnp.bfloat16)

    part_other = project(n_core - 1 - c)
    got = lax.ppermute(part_other, "core", perm=[(0, 1), (1, 0)])
    part_own = lax.optimization_barrier(project(c))
    half = (part_own.astype(jnp.float32) + got.astype(jnp.float32)).astype(jnp.bfloat16)
    return lax.psum_scatter(half, "z", scatter_dimension=0, tiled=True)

def solution(mesh):
    n_seq, n_tp = mesh.devices.shape
    n_x = 4
    mesh4 = Mesh(mesh.devices.reshape(n_seq // n_x, n_x, n_tp // 2, 2), ("y", "x", "z", "core"))
    seq = ("y", "x")
    tp = ("z", "core")
    return jax.shard_map(
        shards,
        mesh=mesh4,
        in_specs=(
            P(),
            P(),
            P(seq, tp),
            P(seq + tp, None),
            P(seq + tp, None),
            P(tp, None),
        ),
        out_specs=P(seq + tp, None),
        check_vma=False,
    )
```

```python
import functools

import jax
import jax.numpy as jnp
import numpy as np
from jax import lax
from jax.experimental import pallas as pl
from jax.experimental.pallas import tpu as pltpu
from jax.sharding import Mesh
from jax.sharding import PartitionSpec as P

QH = 32
KVH = 4
HD = 128
MOST_LEN = 2048


TILE = 256


def _attention_body(scale, n_pieces, n_tiles, flags_ref, q_ref, *refs):
    kv_refs = refs[:n_pieces]
    qp_ref, qs_ref, kp_ref, ks_ref, o_ref, m_ref, l_ref, acc_ref = refs[n_pieces:]
    q = q_ref[...]
    qp = qp_ref[...]
    qs = qs_ref[...]

    def scores(p, j):
        k = kv_refs[p][pl.ds(j * TILE, TILE), pl.ds(0, HD)]
        s = lax.dot_general(q, k, (((1,), (1,)), ((), ())), preferred_element_type=jnp.float32) * scale
        kp = kp_ref[pl.ds(p, 1), pl.ds(j * TILE, TILE)]
        ks = ks_ref[pl.ds(p, 1), pl.ds(j * TILE, TILE)]
        live = (kp <= qp) & (ks == qs)
        return s, live

    m_ref[...] = jnp.full(m_ref.shape, -1e30, jnp.float32)
    l_ref[...] = jnp.zeros(l_ref.shape, jnp.float32)
    acc_ref[...] = jnp.zeros(acc_ref.shape, jnp.float32)
    for p in range(n_pieces):
        for j in range(n_tiles):
            @pl.when(flags_ref[p * n_tiles + j] > 0)
            def _():
                s, live = scores(p, j)
                masked = jnp.where(live, s, jnp.float32(-1e30))
                m_ref[...] = jnp.maximum(m_ref[...], jnp.max(masked, axis=1, keepdims=True))
    for p in range(n_pieces):
        for j in range(n_tiles):
            @pl.when(flags_ref[p * n_tiles + j] > 0)
            def _():
                s, live = scores(p, j)
                expo = jnp.where(live, jnp.exp(s - m_ref[...]), jnp.float32(0.0))
                l_ref[...] += jnp.sum(expo, axis=1, keepdims=True)
                v = kv_refs[p][pl.ds(j * TILE, TILE), pl.ds(HD, HD)]
                acc_ref[...] += jnp.dot(expo.astype(jnp.bfloat16), v, preferred_element_type=jnp.float32)
    o_ref[...] = (acc_ref[...] / l_ref[...]).astype(o_ref.dtype)


def attention(q, pieces, q_pos, q_seg, k_pos, k_seg, scale):
    rows, width = q.shape
    heads = width // HD
    n_pieces = len(pieces)
    n = pieces[0].shape[0]
    n_tiles = n // TILE
    kp_t = k_pos.reshape(n_pieces, n_tiles, TILE)
    ks_t = k_seg.reshape(n_pieces, n_tiles, TILE)
    flags = (
        (kp_t[:, :, 0] <= q_pos[-1])
        & (ks_t[:, :, -1] >= q_seg[0])
        & (ks_t[:, :, 0] <= q_seg[-1])
    ).astype(jnp.int32).reshape(-1)
    grid_spec = pltpu.PrefetchScalarGridSpec(
        num_scalar_prefetch=1,
        grid=(heads,),
        in_specs=[pl.BlockSpec((rows, HD), lambda h, f: (0, h))]
        + [pl.BlockSpec((n, 2 * HD), lambda h, f: (0, 0)) for _ in range(n_pieces)]
        + [
            pl.BlockSpec((rows, 1), lambda h, f: (0, 0)),
            pl.BlockSpec((rows, 1), lambda h, f: (0, 0)),
            pl.BlockSpec((n_pieces, n), lambda h, f: (0, 0)),
            pl.BlockSpec((n_pieces, n), lambda h, f: (0, 0)),
        ],
        out_specs=pl.BlockSpec((rows, HD), lambda h, f: (0, h)),
        scratch_shapes=[
            pltpu.VMEM((rows, 1), jnp.float32),
            pltpu.VMEM((rows, 1), jnp.float32),
            pltpu.VMEM((rows, HD), jnp.float32),
        ],
    )
    return pl.pallas_call(
        functools.partial(_attention_body, scale, n_pieces, n_tiles),
        grid_spec=grid_spec,
        out_shape=jax.ShapeDtypeStruct((rows, width), jnp.bfloat16),
        cost_estimate=pl.CostEstimate(
            flops=6 * rows * n * n_pieces * HD * heads,
            transcendentals=rows * n * n_pieces * heads,
            bytes_accessed=2 * (2 * rows * width + 2 * n_pieces * n * HD),
        ),
    )(flags, q, *pieces, q_pos.reshape(rows, 1), q_seg.reshape(rows, 1), k_pos, k_seg)


def shards(segment_ids, relayout, queries, keys, values, out_weight):
    rows = queries.shape[0]
    n_seq = lax.axis_size("y") * lax.axis_size("x")
    n_z = lax.axis_size("z")
    n_core = lax.axis_size("core")
    s = lax.axis_index("y") * lax.axis_size("x") + lax.axis_index("x")
    t = lax.axis_index("z") * n_core + lax.axis_index("core")
    heads_here = queries.shape[1] // HD
    group = QH // KVH
    kv_width = keys.shape[1]
    scale = HD ** (-0.5)
    back = -(-(MOST_LEN - 1) // rows)
    back = min(back, n_seq - 1)

    n_tp = n_z * n_core
    kv_heads = kv_width // HD
    n_x = lax.axis_size("x")
    heads_of = np.tile(np.arange(n_tp) * heads_here // group, n_x)
    k_h = jnp.transpose(keys.reshape(keys.shape[0], kv_heads, HD), (1, 0, 2))
    v_h = jnp.transpose(values.reshape(values.shape[0], kv_heads, HD), (1, 0, 2))
    pieces = jnp.concatenate([k_h, v_h], axis=2)[heads_of]
    row = lax.all_to_all(pieces, ("x", "z", "core"), split_axis=0, concat_axis=0, tiled=True)
    row = row.reshape(n_x * rows, 2 * HD)

    n_y = lax.axis_size("y")
    x = lax.axis_index("x")
    c = lax.axis_index("core")
    rows_back = -(-back // n_x)
    assert rows_back == n_core
    perm = []
    for cc in range(n_core):
        k = cc + 1
        if k <= rows_back:
            perm += [(yy * n_core + cc, (yy + k) * n_core + cc) for yy in range(n_y - k)]
    fetched = lax.ppermute(row, ("y", "core"), perm=perm)
    swapped = lax.ppermute(fetched, "core", perm=[(i, (i + 1) % n_core) for i in range(n_core)])
    y = lax.axis_index("y")
    span = n_x * rows
    piece_rows = [y - 1 - c, y - n_core + c, y]
    k_pos = jnp.stack([r * span + jnp.arange(span, dtype=jnp.int32) for r in piece_rows])
    pad = rows_back * span
    seg_pad = jnp.concatenate([jnp.full((pad,), -1, jnp.int32), segment_ids])
    k_seg = jnp.stack([lax.dynamic_slice_in_dim(seg_pad, r * span + pad, span, 0) for r in piece_rows])
    q_pos = s * rows + jnp.arange(rows, dtype=jnp.int32)
    q_seg = lax.dynamic_slice_in_dim(segment_ids, s * rows, rows, 0)
    attn_rows = attention(queries, [fetched, swapped, row], q_pos, q_seg, k_pos, k_seg, scale)

    chunk = rows // n_seq
    total = relayout.shape[0]
    here = s * rows + jnp.arange(rows, dtype=jnp.int32)
    new_of = jnp.sum(
        jnp.where(relayout[None, :] == here[:, None], jnp.arange(total, dtype=jnp.int32)[None, :], 0),
        axis=1,
    )
    rank = jnp.sum((new_of[None, :] < new_of[:, None]).astype(jnp.int32), axis=1)
    send_sel = (rank[None, :] == jnp.arange(rows, dtype=jnp.int32)[:, None]).astype(jnp.bfloat16)
    to_send = jnp.dot(send_sel, attn_rows, preferred_element_type=jnp.float32).astype(jnp.bfloat16)
    arrived = lax.all_to_all(to_send, ("y", "x"), split_axis=0, concat_axis=0, tiled=True)

    src = lax.dynamic_slice_in_dim(relayout, s * rows, rows, 0) // rows
    before = jnp.arange(rows)[None, :] < jnp.arange(rows)[:, None]
    nth = jnp.sum((before & (src[None, :] == src[:, None])).astype(jnp.int32), axis=1)
    slot = src * chunk + nth
    per_dev = rows // (n_z * n_core)
    slot3 = slot.reshape(n_z, n_core, per_dev)
    cols = jnp.arange(rows, dtype=jnp.int32)[None, :]

    def project(which):
        chosen = jnp.take(slot3, which, axis=1).reshape(-1)
        sel = (chosen[:, None] == cols).astype(jnp.bfloat16)
        relaid = jnp.dot(sel, arrived, preferred_element_type=jnp.float32).astype(jnp.bfloat16)
        return jnp.dot(relaid, out_weight, preferred_element_type=jnp.float32).astype(jnp.bfloat16)

    part_other = project(n_core - 1 - c)
    got = lax.ppermute(part_other, "core", perm=[(0, 1), (1, 0)])
    part_own = lax.optimization_barrier(project(c))
    half = (part_own.astype(jnp.float32) + got.astype(jnp.float32)).astype(jnp.bfloat16)
    return lax.psum_scatter(half, "z", scatter_dimension=0, tiled=True)

def solution(mesh):
    n_seq, n_tp = mesh.devices.shape
    n_x = 4
    mesh4 = Mesh(mesh.devices.reshape(n_seq // n_x, n_x, n_tp // 2, 2), ("y", "x", "z", "core"))
    seq = ("y", "x")
    tp = ("z", "core")
    return jax.shard_map(
        shards,
        mesh=mesh4,
        in_specs=(
            P(),
            P(),
            P(seq, tp),
            P(seq + tp, None),
            P(seq + tp, None),
            P(tp, None),
        ),
        out_specs=P(seq + tp, None),
        check_vma=False,
    )
```

```python
import functools

import jax
import jax.numpy as jnp
import numpy as np
from jax import lax
from jax.experimental import pallas as pl
from jax.experimental.pallas import tpu as pltpu
from jax.sharding import Mesh
from jax.sharding import PartitionSpec as P

QH = 32
KVH = 4
HD = 128
MOST_LEN = 2048


TILE = 256


def _attention_body(scale, n_pieces, n_tiles, carry_in, final, flags_ref, q_ref, *refs):
    kv_refs = refs[:n_pieces]
    refs = refs[n_pieces:]
    qp_ref, qs_ref, kp_ref, ks_ref = refs[:4]
    refs = refs[4:]
    if carry_in:
        m_in, l_in, acc_in = refs[:3]
        refs = refs[3:]
    if final:
        o_ref, m_ref, l_ref, acc_ref = refs
    else:
        m_ref, l_ref, acc_ref = refs
    q = q_ref[...]
    qp = qp_ref[...]
    qs = qs_ref[...]
    if carry_in:
        m_ref[0] = m_in[0]
        l_ref[0] = l_in[0]
        acc_ref[...] = acc_in[...]
    else:
        m_ref[...] = jnp.full(m_ref.shape, -1e30, jnp.float32)
        l_ref[...] = jnp.zeros(l_ref.shape, jnp.float32)
        acc_ref[...] = jnp.zeros(acc_ref.shape, jnp.float32)
    for p in range(n_pieces):
        for j in range(n_tiles):
            @pl.when(flags_ref[p * n_tiles + j] > 0)
            def _():
                k = kv_refs[p][pl.ds(j * TILE, TILE), pl.ds(0, HD)]
                s = lax.dot_general(q, k, (((1,), (1,)), ((), ())), preferred_element_type=jnp.float32) * scale
                kp = kp_ref[pl.ds(p, 1), pl.ds(j * TILE, TILE)]
                ks = ks_ref[pl.ds(p, 1), pl.ds(j * TILE, TILE)]
                live = (kp <= qp) & (ks == qs)
                m_old = m_ref[0]
                m_new = jnp.maximum(m_old, jnp.max(jnp.where(live, s, jnp.float32(-1e30)), axis=1, keepdims=True))
                alpha = jnp.exp(m_old - m_new)
                expo = jnp.where(live, jnp.exp(s - m_new), jnp.float32(0.0))
                l_ref[0] = alpha * l_ref[0] + jnp.sum(expo, axis=1, keepdims=True)
                v = kv_refs[p][pl.ds(j * TILE, TILE), pl.ds(HD, HD)]
                acc_ref[...] = alpha * acc_ref[...] + jnp.dot(
                    expo.astype(jnp.bfloat16), v, preferred_element_type=jnp.float32
                )
                m_ref[0] = m_new
    if final:
        o_ref[...] = (acc_ref[...] / l_ref[0]).astype(o_ref.dtype)


def attention(q, pieces, q_pos, q_seg, k_pos, k_seg, scale, carry=None, final=True):
    rows, width = q.shape
    heads = width // HD
    n_pieces = len(pieces)
    n = pieces[0].shape[0]
    n_tiles = n // TILE
    kp_t = k_pos.reshape(n_pieces, n_tiles, TILE)
    ks_t = k_seg.reshape(n_pieces, n_tiles, TILE)
    flags = (
        (kp_t[:, :, 0] <= q_pos[-1]) & (ks_t[:, :, -1] >= q_seg[0]) & (ks_t[:, :, 0] <= q_seg[-1])
    ).astype(jnp.int32).reshape(-1)
    stat_spec = pl.BlockSpec((1, rows, 1), lambda h, f: (h, 0, 0))
    acc_spec = pl.BlockSpec((rows, HD), lambda h, f: (0, h))
    in_specs = (
        [pl.BlockSpec((rows, HD), lambda h, f: (0, h))]
        + [pl.BlockSpec((n, 2 * HD), lambda h, f: (0, 0)) for _ in range(n_pieces)]
        + [
            pl.BlockSpec((rows, 1), lambda h, f: (0, 0)),
            pl.BlockSpec((rows, 1), lambda h, f: (0, 0)),
            pl.BlockSpec((n_pieces, n), lambda h, f: (0, 0)),
            pl.BlockSpec((n_pieces, n), lambda h, f: (0, 0)),
        ]
    )
    args = [q, *pieces, q_pos.reshape(rows, 1), q_seg.reshape(rows, 1), k_pos, k_seg]
    if carry is not None:
        in_specs += [stat_spec, stat_spec, acc_spec]
        args += list(carry)
    stat_shape = jax.ShapeDtypeStruct((heads, rows, 1), jnp.float32)
    acc_shape = jax.ShapeDtypeStruct((rows, width), jnp.float32)
    if final:
        out_specs = acc_spec
        out_shape = jax.ShapeDtypeStruct((rows, width), jnp.bfloat16)
        scratch = [
            pltpu.VMEM((1, rows, 1), jnp.float32),
            pltpu.VMEM((1, rows, 1), jnp.float32),
            pltpu.VMEM((rows, HD), jnp.float32),
        ]
    else:
        out_specs = [stat_spec, stat_spec, acc_spec]
        out_shape = [stat_shape, stat_shape, acc_shape]
        scratch = []
    grid_spec = pltpu.PrefetchScalarGridSpec(
        num_scalar_prefetch=1,
        grid=(heads,),
        in_specs=in_specs,
        out_specs=out_specs,
        scratch_shapes=scratch,
    )
    return pl.pallas_call(
        functools.partial(_attention_body, scale, n_pieces, n_tiles, carry is not None, final),
        grid_spec=grid_spec,
        out_shape=out_shape,
        cost_estimate=pl.CostEstimate(
            flops=4 * rows * n * n_pieces * HD * heads,
            transcendentals=rows * n * n_pieces * heads,
            bytes_accessed=2 * (2 * rows * width + 2 * n_pieces * n * HD),
        ),
    )(flags, *args)


def shards(segment_ids, relayout, queries, keys, values, out_weight):
    rows = queries.shape[0]
    n_seq = lax.axis_size("y") * lax.axis_size("x")
    n_z = lax.axis_size("z")
    n_core = lax.axis_size("core")
    s = lax.axis_index("y") * lax.axis_size("x") + lax.axis_index("x")
    t = lax.axis_index("z") * n_core + lax.axis_index("core")
    heads_here = queries.shape[1] // HD
    group = QH // KVH
    kv_width = keys.shape[1]
    scale = HD ** (-0.5)
    back = -(-(MOST_LEN - 1) // rows)
    back = min(back, n_seq - 1)

    n_tp = n_z * n_core
    kv_heads = kv_width // HD
    n_x = lax.axis_size("x")
    heads_of = np.tile(np.arange(n_tp) * heads_here // group, n_x)
    k_h = jnp.transpose(keys.reshape(keys.shape[0], kv_heads, HD), (1, 0, 2))
    v_h = jnp.transpose(values.reshape(values.shape[0], kv_heads, HD), (1, 0, 2))
    pieces = jnp.concatenate([k_h, v_h], axis=2)[heads_of]
    row = lax.all_to_all(pieces, ("x", "z", "core"), split_axis=0, concat_axis=0, tiled=True)
    row = row.reshape(n_x * rows, 2 * HD)

    n_y = lax.axis_size("y")
    x = lax.axis_index("x")
    c = lax.axis_index("core")
    rows_back = -(-back // n_x)
    assert rows_back == n_core
    perm = []
    for cc in range(n_core):
        k = cc + 1
        if k <= rows_back:
            perm += [(yy * n_core + cc, (yy + k) * n_core + cc) for yy in range(n_y - k)]
    fetched = lax.ppermute(row, ("y", "core"), perm=perm)
    y = lax.axis_index("y")
    span = n_x * rows
    piece_rows = [y - 1 - c, y - n_core + c, y]
    k_pos = jnp.stack([r * span + jnp.arange(span, dtype=jnp.int32) for r in piece_rows])
    pad = rows_back * span
    seg_pad = jnp.concatenate([jnp.full((pad,), -1, jnp.int32), segment_ids])
    k_seg = jnp.stack([lax.dynamic_slice_in_dim(seg_pad, r * span + pad, span, 0) for r in piece_rows])
    q_pos = s * rows + jnp.arange(rows, dtype=jnp.int32)
    q_seg = lax.dynamic_slice_in_dim(segment_ids, s * rows, rows, 0)
    carry = attention(queries, [row], q_pos, q_seg, k_pos[2:], k_seg[2:], scale, final=False)
    fetched, carry = lax.optimization_barrier((fetched, carry))
    swapped = lax.ppermute(fetched, "core", perm=[(i, (i + 1) % n_core) for i in range(n_core)])
    attn_rows = attention(
        queries, [fetched, swapped], q_pos, q_seg, k_pos[:2], k_seg[:2], scale, carry=carry
    )

    chunk = rows // n_seq
    total = relayout.shape[0]
    here = s * rows + jnp.arange(rows, dtype=jnp.int32)
    new_of = jnp.sum(
        jnp.where(relayout[None, :] == here[:, None], jnp.arange(total, dtype=jnp.int32)[None, :], 0),
        axis=1,
    )
    rank = jnp.sum((new_of[None, :] < new_of[:, None]).astype(jnp.int32), axis=1)
    send_sel = (rank[None, :] == jnp.arange(rows, dtype=jnp.int32)[:, None]).astype(jnp.bfloat16)
    to_send = jnp.dot(send_sel, attn_rows, preferred_element_type=jnp.float32).astype(jnp.bfloat16)
    arrived = lax.all_to_all(to_send, ("y", "x"), split_axis=0, concat_axis=0, tiled=True)

    src = lax.dynamic_slice_in_dim(relayout, s * rows, rows, 0) // rows
    before = jnp.arange(rows)[None, :] < jnp.arange(rows)[:, None]
    nth = jnp.sum((before & (src[None, :] == src[:, None])).astype(jnp.int32), axis=1)
    slot = src * chunk + nth
    per_dev = rows // (n_z * n_core)
    slot3 = slot.reshape(n_z, n_core, per_dev)
    cols = jnp.arange(rows, dtype=jnp.int32)[None, :]

    def project(which):
        chosen = jnp.take(slot3, which, axis=1).reshape(-1)
        sel = (chosen[:, None] == cols).astype(jnp.bfloat16)
        relaid = jnp.dot(sel, arrived, preferred_element_type=jnp.float32).astype(jnp.bfloat16)
        return jnp.dot(relaid, out_weight, preferred_element_type=jnp.float32).astype(jnp.bfloat16)

    part_other = project(n_core - 1 - c)
    got = lax.ppermute(part_other, "core", perm=[(0, 1), (1, 0)])
    part_own = lax.optimization_barrier(project(c))
    half = (part_own.astype(jnp.float32) + got.astype(jnp.float32)).astype(jnp.bfloat16)
    return lax.psum_scatter(half, "z", scatter_dimension=0, tiled=True)

def solution(mesh):
    n_seq, n_tp = mesh.devices.shape
    n_x = 4
    mesh4 = Mesh(mesh.devices.reshape(n_seq // n_x, n_x, n_tp // 2, 2), ("y", "x", "z", "core"))
    seq = ("y", "x")
    tp = ("z", "core")
    return jax.shard_map(
        shards,
        mesh=mesh4,
        in_specs=(
            P(),
            P(),
            P(seq, tp),
            P(seq + tp, None),
            P(seq + tp, None),
            P(tp, None),
        ),
        out_specs=P(seq + tp, None),
        check_vma=False,
    )
```

```python
import functools

import jax
import jax.numpy as jnp
import numpy as np
from jax import lax
from jax.experimental import pallas as pl
from jax.sharding import Mesh
from jax.sharding import PartitionSpec as P

QH = 32
KVH = 4
HD = 128
MOST_LEN = 2048


def _attention_body(scale, n_pieces, heads, carry_in, final, q_ref, *refs):
    kv_refs = refs[:n_pieces]
    refs = refs[n_pieces:]
    qp_ref, qs_ref, kp_ref, ks_ref = refs[:4]
    refs = refs[4:]
    if carry_in:
        m_in, l_in, acc_in = refs[:3]
        refs = refs[3:]
    qp = qp_ref[...]
    qs = qs_ref[...]
    lives = [(kp_ref[pl.ds(p, 1), :] <= qp) & (ks_ref[pl.ds(p, 1), :] == qs) for p in range(n_pieces)]
    for h in range(heads):
        q = q_ref[:, pl.ds(h * HD, HD)]
        scores = [
            jnp.where(
                lives[p],
                lax.dot_general(
                    q, kv_refs[p][:, pl.ds(0, HD)], (((1,), (1,)), ((), ())),
                    preferred_element_type=jnp.float32,
                ) * scale,
                jnp.float32(-1e30),
            )
            for p in range(n_pieces)
        ]
        peak = functools.reduce(jnp.maximum, [jnp.max(s, axis=1, keepdims=True) for s in scores])
        if carry_in:
            peak = jnp.maximum(peak, m_in[h])
        expos = [jnp.where(lives[p], jnp.exp(scores[p] - peak), jnp.float32(0.0)) for p in range(n_pieces)]
        denom = functools.reduce(jnp.add, [jnp.sum(e, axis=1, keepdims=True) for e in expos])
        summed = functools.reduce(
            jnp.add,
            [
                jnp.dot(expos[p].astype(jnp.bfloat16), kv_refs[p][:, pl.ds(HD, HD)], preferred_element_type=jnp.float32)
                for p in range(n_pieces)
            ],
        )
        if carry_in:
            alpha = jnp.exp(m_in[h] - peak)
            denom = denom + alpha * l_in[h]
            summed = summed + alpha * acc_in[:, pl.ds(h * HD, HD)]
        if final:
            refs[0][:, pl.ds(h * HD, HD)] = (summed / denom).astype(refs[0].dtype)
        else:
            refs[0][h] = peak
            refs[1][h] = denom
            refs[2][:, pl.ds(h * HD, HD)] = summed


def attention(q, pieces, q_pos, q_seg, k_pos, k_seg, scale, carry=None, final=True):
    rows, width = q.shape
    heads = width // HD
    n_pieces = len(pieces)
    n = pieces[0].shape[0]
    args = [q, *pieces, q_pos.reshape(rows, 1), q_seg.reshape(rows, 1), k_pos, k_seg]
    if carry is not None:
        args += list(carry)
    if final:
        out_shape = jax.ShapeDtypeStruct((rows, width), jnp.bfloat16)
    else:
        out_shape = [
            jax.ShapeDtypeStruct((heads, rows, 1), jnp.float32),
            jax.ShapeDtypeStruct((heads, rows, 1), jnp.float32),
            jax.ShapeDtypeStruct((rows, width), jnp.float32),
        ]
    return pl.pallas_call(
        functools.partial(_attention_body, scale, n_pieces, heads, carry is not None, final),
        out_shape=out_shape,
        cost_estimate=pl.CostEstimate(
            flops=4 * rows * n * n_pieces * HD * heads,
            transcendentals=rows * n * n_pieces * heads,
            bytes_accessed=2 * (2 * rows * width + 2 * n_pieces * n * HD),
        ),
    )(*args)


def shards(segment_ids, relayout, queries, keys, values, out_weight):
    rows = queries.shape[0]
    n_seq = lax.axis_size("y") * lax.axis_size("x")
    n_z = lax.axis_size("z")
    n_core = lax.axis_size("core")
    s = lax.axis_index("y") * lax.axis_size("x") + lax.axis_index("x")
    t = lax.axis_index("z") * n_core + lax.axis_index("core")
    heads_here = queries.shape[1] // HD
    group = QH // KVH
    kv_width = keys.shape[1]
    scale = HD ** (-0.5)
    back = -(-(MOST_LEN - 1) // rows)
    back = min(back, n_seq - 1)

    n_tp = n_z * n_core
    kv_heads = kv_width // HD
    n_x = lax.axis_size("x")
    heads_of = np.tile(np.arange(n_tp) * heads_here // group, n_x)
    k_h = jnp.transpose(keys.reshape(keys.shape[0], kv_heads, HD), (1, 0, 2))
    v_h = jnp.transpose(values.reshape(values.shape[0], kv_heads, HD), (1, 0, 2))
    pieces = jnp.concatenate([k_h, v_h], axis=2)[heads_of]
    row = lax.all_to_all(pieces, ("x", "z", "core"), split_axis=0, concat_axis=0, tiled=True)
    row = row.reshape(n_x * rows, 2 * HD)

    n_y = lax.axis_size("y")
    x = lax.axis_index("x")
    c = lax.axis_index("core")
    rows_back = -(-back // n_x)
    assert rows_back == n_core
    perm = []
    for cc in range(n_core):
        k = cc + 1
        if k <= rows_back:
            perm += [(yy * n_core + cc, (yy + k) * n_core + cc) for yy in range(n_y - k)]
    fetched = lax.ppermute(row, ("y", "core"), perm=perm)
    y = lax.axis_index("y")
    span = n_x * rows
    piece_rows = [y - 1 - c, y - n_core + c, y]
    k_pos = jnp.stack([r * span + jnp.arange(span, dtype=jnp.int32) for r in piece_rows])
    pad = rows_back * span
    seg_pad = jnp.concatenate([jnp.full((pad,), -1, jnp.int32), segment_ids])
    k_seg = jnp.stack([lax.dynamic_slice_in_dim(seg_pad, r * span + pad, span, 0) for r in piece_rows])
    q_pos = s * rows + jnp.arange(rows, dtype=jnp.int32)
    q_seg = lax.dynamic_slice_in_dim(segment_ids, s * rows, rows, 0)
    carry = attention(queries, [row], q_pos, q_seg, k_pos[2:], k_seg[2:], scale, final=False)
    fetched, carry = lax.optimization_barrier((fetched, carry))
    swapped = lax.ppermute(fetched, "core", perm=[(i, (i + 1) % n_core) for i in range(n_core)])
    attn_rows = attention(
        queries, [fetched, swapped], q_pos, q_seg, k_pos[:2], k_seg[:2], scale, carry=carry
    )

    chunk = rows // n_seq
    total = relayout.shape[0]
    here = s * rows + jnp.arange(rows, dtype=jnp.int32)
    new_of = jnp.sum(
        jnp.where(relayout[None, :] == here[:, None], jnp.arange(total, dtype=jnp.int32)[None, :], 0),
        axis=1,
    )
    rank = jnp.sum((new_of[None, :] < new_of[:, None]).astype(jnp.int32), axis=1)
    send_sel = (rank[None, :] == jnp.arange(rows, dtype=jnp.int32)[:, None]).astype(jnp.bfloat16)
    to_send = jnp.dot(send_sel, attn_rows, preferred_element_type=jnp.float32).astype(jnp.bfloat16)
    arrived = lax.all_to_all(to_send, ("y", "x"), split_axis=0, concat_axis=0, tiled=True)

    src = lax.dynamic_slice_in_dim(relayout, s * rows, rows, 0) // rows
    before = jnp.arange(rows)[None, :] < jnp.arange(rows)[:, None]
    nth = jnp.sum((before & (src[None, :] == src[:, None])).astype(jnp.int32), axis=1)
    slot = src * chunk + nth
    per_dev = rows // (n_z * n_core)
    slot3 = slot.reshape(n_z, n_core, per_dev)
    cols = jnp.arange(rows, dtype=jnp.int32)[None, :]

    def project(which):
        chosen = jnp.take(slot3, which, axis=1).reshape(-1)
        sel = (chosen[:, None] == cols).astype(jnp.bfloat16)
        relaid = jnp.dot(sel, arrived, preferred_element_type=jnp.float32).astype(jnp.bfloat16)
        return jnp.dot(relaid, out_weight, preferred_element_type=jnp.float32).astype(jnp.bfloat16)

    part_other = project(n_core - 1 - c)
    got = lax.ppermute(part_other, "core", perm=[(0, 1), (1, 0)])
    part_own = lax.optimization_barrier(project(c))
    half = (part_own.astype(jnp.float32) + got.astype(jnp.float32)).astype(jnp.bfloat16)
    return lax.psum_scatter(half, "z", scatter_dimension=0, tiled=True)

def solution(mesh):
    n_seq, n_tp = mesh.devices.shape
    n_x = 4
    mesh4 = Mesh(mesh.devices.reshape(n_seq // n_x, n_x, n_tp // 2, 2), ("y", "x", "z", "core"))
    seq = ("y", "x")
    tp = ("z", "core")
    return jax.shard_map(
        shards,
        mesh=mesh4,
        in_specs=(
            P(),
            P(),
            P(seq, tp),
            P(seq + tp, None),
            P(seq + tp, None),
            P(tp, None),
        ),
        out_specs=P(seq + tp, None),
        check_vma=False,
    )
```

```python
import functools

import jax
import jax.numpy as jnp
import numpy as np
from jax import lax
from jax.experimental import pallas as pl
from jax.sharding import Mesh
from jax.sharding import PartitionSpec as P

QH = 32
KVH = 4
HD = 128
MOST_LEN = 2048


def _attention_body(scale, n_pieces, heads, carry_in, final, q_ref, *refs):
    kv_refs = refs[:n_pieces]
    refs = refs[n_pieces:]
    qp_ref, qs_ref, kp_ref, ks_ref = refs[:4]
    refs = refs[4:]
    if carry_in:
        m_in, l_in, acc_in = refs[:3]
        refs = refs[3:]
    qp = qp_ref[...]
    qs = qs_ref[...]
    lives = [(kp_ref[pl.ds(p, 1), :] <= qp) & (ks_ref[pl.ds(p, 1), :] == qs) for p in range(n_pieces)]
    for h in range(heads):
        q = q_ref[:, pl.ds(h * HD, HD)]
        scores = [
            jnp.where(
                lives[p],
                lax.dot_general(
                    q, kv_refs[p][:, pl.ds(0, HD)], (((1,), (1,)), ((), ())),
                    preferred_element_type=jnp.float32,
                ) * scale,
                jnp.float32(-1e30),
            )
            for p in range(n_pieces)
        ]
        peak = functools.reduce(jnp.maximum, [jnp.max(s, axis=1, keepdims=True) for s in scores])
        if carry_in:
            peak = jnp.maximum(peak, m_in[h])
        expos = [jnp.where(lives[p], jnp.exp(scores[p] - peak), jnp.float32(0.0)) for p in range(n_pieces)]
        denom = functools.reduce(jnp.add, [jnp.sum(e, axis=1, keepdims=True) for e in expos])
        summed = functools.reduce(
            jnp.add,
            [
                jnp.dot(expos[p].astype(jnp.bfloat16), kv_refs[p][:, pl.ds(HD, HD)], preferred_element_type=jnp.float32)
                for p in range(n_pieces)
            ],
        )
        if carry_in:
            alpha = jnp.exp(m_in[h] - peak)
            denom = denom + alpha * l_in[h]
            summed = summed + alpha * acc_in[:, pl.ds(h * HD, HD)]
        if final:
            refs[0][:, pl.ds(h * HD, HD)] = (summed / denom).astype(refs[0].dtype)
        else:
            refs[0][h] = peak
            refs[1][h] = denom
            refs[2][:, pl.ds(h * HD, HD)] = summed


def attention(q, pieces, q_pos, q_seg, k_pos, k_seg, scale, carry=None, final=True):
    rows, width = q.shape
    heads = width // HD
    n_pieces = len(pieces)
    n = pieces[0].shape[0]
    args = [q, *pieces, q_pos.reshape(rows, 1), q_seg.reshape(rows, 1), k_pos, k_seg]
    if carry is not None:
        args += list(carry)
    if final:
        out_shape = jax.ShapeDtypeStruct((rows, width), jnp.bfloat16)
    else:
        out_shape = [
            jax.ShapeDtypeStruct((heads, rows, 1), jnp.float32),
            jax.ShapeDtypeStruct((heads, rows, 1), jnp.float32),
            jax.ShapeDtypeStruct((rows, width), jnp.float32),
        ]
    return pl.pallas_call(
        functools.partial(_attention_body, scale, n_pieces, heads, carry is not None, final),
        out_shape=out_shape,
        cost_estimate=pl.CostEstimate(
            flops=4 * rows * n * n_pieces * HD * heads,
            transcendentals=rows * n * n_pieces * heads,
            bytes_accessed=2 * (2 * rows * width + 2 * n_pieces * n * HD),
        ),
    )(*args)


def shards(segment_ids, relayout, queries, keys, values, out_weight):
    rows = queries.shape[0]
    n_seq = lax.axis_size("y") * lax.axis_size("x")
    n_z = lax.axis_size("z")
    n_core = lax.axis_size("core")
    s = lax.axis_index("y") * lax.axis_size("x") + lax.axis_index("x")
    t = lax.axis_index("z") * n_core + lax.axis_index("core")
    heads_here = queries.shape[1] // HD
    group = QH // KVH
    kv_width = keys.shape[1]
    scale = HD ** (-0.5)
    back = -(-(MOST_LEN - 1) // rows)
    back = min(back, n_seq - 1)

    n_tp = n_z * n_core
    kv_heads = kv_width // HD
    n_x = lax.axis_size("x")
    heads_of = np.tile(np.arange(n_tp) * heads_here // group, n_x)
    k_h = jnp.transpose(keys.reshape(keys.shape[0], kv_heads, HD), (1, 0, 2))
    v_h = jnp.transpose(values.reshape(values.shape[0], kv_heads, HD), (1, 0, 2))
    pieces = jnp.concatenate([k_h, v_h], axis=2)[heads_of]
    row = lax.all_to_all(pieces, ("x", "z", "core"), split_axis=0, concat_axis=0, tiled=True)
    row = row.reshape(n_x * rows, 2 * HD)

    n_y = lax.axis_size("y")
    x = lax.axis_index("x")
    c = lax.axis_index("core")
    rows_back = -(-back // n_x)
    assert rows_back == n_core
    perm = []
    for cc in range(n_core):
        k = cc + 1
        if k <= rows_back:
            perm += [(yy * n_core + cc, (yy + k) * n_core + cc) for yy in range(n_y - k)]
    fetched = lax.ppermute(row, ("y", "core"), perm=perm)
    y = lax.axis_index("y")
    span = n_x * rows
    piece_rows = [y - 1 - c, y - n_core + c, y]
    k_pos = jnp.stack([r * span + jnp.arange(span, dtype=jnp.int32) for r in piece_rows])
    pad = rows_back * span
    seg_pad = jnp.concatenate([jnp.full((pad,), -1, jnp.int32), segment_ids])
    k_seg = jnp.stack([lax.dynamic_slice_in_dim(seg_pad, r * span + pad, span, 0) for r in piece_rows])
    q_pos = s * rows + jnp.arange(rows, dtype=jnp.int32)
    q_seg = lax.dynamic_slice_in_dim(segment_ids, s * rows, rows, 0)
    chunk = rows // n_seq
    total = relayout.shape[0]
    here = s * rows + jnp.arange(rows, dtype=jnp.int32)
    new_of = jnp.sum(
        jnp.where(relayout[None, :] == here[:, None], jnp.arange(total, dtype=jnp.int32)[None, :], 0),
        axis=1,
    )
    rank = jnp.sum((new_of[None, :] < new_of[:, None]).astype(jnp.int32), axis=1)
    send_hit = rank[None, :] == jnp.arange(rows, dtype=jnp.int32)[:, None]
    q_sent = jnp.dot(send_hit.astype(jnp.bfloat16), queries, preferred_element_type=jnp.float32).astype(jnp.bfloat16)
    q_pos = jnp.sum(jnp.where(send_hit, here[None, :], 0), axis=1)
    q_seg = jnp.sum(jnp.where(send_hit, q_seg[None, :], 0), axis=1)
    carry = attention(q_sent, [row], q_pos, q_seg, k_pos[2:], k_seg[2:], scale, final=False)
    fetched, carry = lax.optimization_barrier((fetched, carry))
    swapped = lax.ppermute(fetched, "core", perm=[(i, (i + 1) % n_core) for i in range(n_core)])
    to_send = attention(
        q_sent, [fetched, swapped], q_pos, q_seg, k_pos[:2], k_seg[:2], scale, carry=carry
    )

    arrived = lax.all_to_all(to_send, ("y", "x"), split_axis=0, concat_axis=0, tiled=True)

    src = lax.dynamic_slice_in_dim(relayout, s * rows, rows, 0) // rows
    before = jnp.arange(rows)[None, :] < jnp.arange(rows)[:, None]
    nth = jnp.sum((before & (src[None, :] == src[:, None])).astype(jnp.int32), axis=1)
    slot = src * chunk + nth
    per_dev = rows // (n_z * n_core)
    slot3 = slot.reshape(n_z, n_core, per_dev)
    cols = jnp.arange(rows, dtype=jnp.int32)[None, :]

    def project(which):
        chosen = jnp.take(slot3, which, axis=1).reshape(-1)
        sel = (chosen[:, None] == cols).astype(jnp.bfloat16)
        relaid = jnp.dot(sel, arrived, preferred_element_type=jnp.float32).astype(jnp.bfloat16)
        return jnp.dot(relaid, out_weight, preferred_element_type=jnp.float32).astype(jnp.bfloat16)

    part_other = project(n_core - 1 - c)
    got = lax.ppermute(part_other, "core", perm=[(0, 1), (1, 0)])
    part_own = lax.optimization_barrier(project(c))
    half = (part_own.astype(jnp.float32) + got.astype(jnp.float32)).astype(jnp.bfloat16)
    return lax.psum_scatter(half, "z", scatter_dimension=0, tiled=True)

def solution(mesh):
    n_seq, n_tp = mesh.devices.shape
    n_x = 4
    mesh4 = Mesh(mesh.devices.reshape(n_seq // n_x, n_x, n_tp // 2, 2), ("y", "x", "z", "core"))
    seq = ("y", "x")
    tp = ("z", "core")
    return jax.shard_map(
        shards,
        mesh=mesh4,
        in_specs=(
            P(),
            P(),
            P(seq, tp),
            P(seq + tp, None),
            P(seq + tp, None),
            P(tp, None),
        ),
        out_specs=P(seq + tp, None),
        check_vma=False,
    )
```

```python
import functools

import jax
import jax.numpy as jnp
import numpy as np
from jax import lax
from jax.experimental import pallas as pl
from jax.sharding import Mesh
from jax.sharding import PartitionSpec as P

QH = 32
KVH = 4
HD = 128
MOST_LEN = 2048


def _attention_body(scale, n_pieces, heads, carry_in, final, q_ref, *refs):
    kv_refs = refs[:n_pieces]
    refs = refs[n_pieces:]
    qp_ref, qs_ref, kp_ref, ks_ref = refs[:4]
    refs = refs[4:]
    if carry_in:
        m_in, l_in, acc_in = refs[:3]
        refs = refs[3:]
    qp = qp_ref[...]
    qs = qs_ref[...]
    lives = [(kp_ref[pl.ds(p, 1), :] <= qp) & (ks_ref[pl.ds(p, 1), :] == qs) for p in range(n_pieces)]
    for h in range(heads):
        q = q_ref[:, pl.ds(h * HD, HD)]
        scores = [
            jnp.where(
                lives[p],
                lax.dot_general(
                    q, kv_refs[p][:, pl.ds(0, HD)], (((1,), (1,)), ((), ())),
                    preferred_element_type=jnp.float32,
                ) * scale,
                jnp.float32(-1e30),
            )
            for p in range(n_pieces)
        ]
        peak = functools.reduce(jnp.maximum, [jnp.max(s, axis=1, keepdims=True) for s in scores])
        if carry_in:
            peak = jnp.maximum(peak, m_in[h])
        expos = [jnp.where(lives[p], jnp.exp(scores[p] - peak), jnp.float32(0.0)) for p in range(n_pieces)]
        denom = functools.reduce(jnp.add, [jnp.sum(e, axis=1, keepdims=True) for e in expos])
        summed = functools.reduce(
            jnp.add,
            [
                jnp.dot(expos[p].astype(jnp.bfloat16), kv_refs[p][:, pl.ds(HD, HD)], preferred_element_type=jnp.float32)
                for p in range(n_pieces)
            ],
        )
        if carry_in:
            alpha = jnp.exp(m_in[h] - peak)
            denom = denom + alpha * l_in[h]
            summed = summed + alpha * acc_in[:, pl.ds(h * HD, HD)]
        if final:
            refs[0][:, pl.ds(h * HD, HD)] = (summed / denom).astype(refs[0].dtype)
        else:
            refs[0][h] = peak
            refs[1][h] = denom
            refs[2][:, pl.ds(h * HD, HD)] = summed


def attention(q, pieces, q_pos, q_seg, k_pos, k_seg, scale, carry=None, final=True):
    rows, width = q.shape
    heads = width // HD
    n_pieces = len(pieces)
    n = pieces[0].shape[0]
    args = [q, *pieces, q_pos.reshape(rows, 1), q_seg.reshape(rows, 1), k_pos, k_seg]
    if carry is not None:
        args += list(carry)
    if final:
        out_shape = jax.ShapeDtypeStruct((rows, width), jnp.bfloat16)
    else:
        out_shape = [
            jax.ShapeDtypeStruct((heads, rows, 1), jnp.float32),
            jax.ShapeDtypeStruct((heads, rows, 1), jnp.float32),
            jax.ShapeDtypeStruct((rows, width), jnp.float32),
        ]
    return pl.pallas_call(
        functools.partial(_attention_body, scale, n_pieces, heads, carry is not None, final),
        out_shape=out_shape,
        cost_estimate=pl.CostEstimate(
            flops=4 * rows * n * n_pieces * HD * heads,
            transcendentals=rows * n * n_pieces * heads,
            bytes_accessed=2 * (2 * rows * width + 2 * n_pieces * n * HD),
        ),
    )(*args)


def shards(segment_ids, relayout, queries, keys, values, out_weight):
    rows = queries.shape[0]
    n_seq = lax.axis_size("y") * lax.axis_size("x")
    n_z = lax.axis_size("z")
    n_core = lax.axis_size("core")
    s = lax.axis_index("y") * lax.axis_size("x") + lax.axis_index("x")
    t = lax.axis_index("z") * n_core + lax.axis_index("core")
    heads_here = queries.shape[1] // HD
    group = QH // KVH
    kv_width = keys.shape[1]
    scale = HD ** (-0.5)
    back = -(-(MOST_LEN - 1) // rows)
    back = min(back, n_seq - 1)

    n_tp = n_z * n_core
    kv_heads = kv_width // HD
    n_x = lax.axis_size("x")
    heads_of = np.tile(np.arange(n_tp) * heads_here // group, n_x)
    k_h = jnp.transpose(keys.reshape(keys.shape[0], kv_heads, HD), (1, 0, 2))
    v_h = jnp.transpose(values.reshape(values.shape[0], kv_heads, HD), (1, 0, 2))
    pieces = jnp.concatenate([k_h, v_h], axis=2)[heads_of]
    row = lax.all_to_all(pieces, ("x", "z", "core"), split_axis=0, concat_axis=0, tiled=True)
    row = row.reshape(n_x * rows, 2 * HD)

    n_y = lax.axis_size("y")
    x = lax.axis_index("x")
    c = lax.axis_index("core")
    rows_back = -(-back // n_x)
    assert rows_back == n_core
    perm = []
    for cc in range(n_core):
        k = cc + 1
        if k <= rows_back:
            perm += [(yy * n_core + cc, (yy + k) * n_core + cc) for yy in range(n_y - k)]
    fetched = lax.ppermute(row, ("y", "core"), perm=perm)
    y = lax.axis_index("y")
    span = n_x * rows
    piece_rows = [y - 1 - c, y - n_core + c, y]
    k_pos = jnp.stack([r * span + jnp.arange(span, dtype=jnp.int32) for r in piece_rows])
    pad = rows_back * span
    seg_pad = jnp.concatenate([jnp.full((pad,), -1, jnp.int32), segment_ids])
    k_seg = jnp.stack([lax.dynamic_slice_in_dim(seg_pad, r * span + pad, span, 0) for r in piece_rows])
    q_pos = s * rows + jnp.arange(rows, dtype=jnp.int32)
    q_seg = lax.dynamic_slice_in_dim(segment_ids, s * rows, rows, 0)
    chunk = rows // n_seq
    total = relayout.shape[0]
    here = s * rows + jnp.arange(rows, dtype=jnp.int32)
    new_of = jnp.sum(
        jnp.where(relayout[None, :] == here[:, None], jnp.arange(total, dtype=jnp.int32)[None, :], 0),
        axis=1,
    )
    rank = jnp.sum((new_of[None, :] < new_of[:, None]).astype(jnp.int32), axis=1)
    send_hit = rank[None, :] == jnp.arange(rows, dtype=jnp.int32)[:, None]
    q_sent = jnp.dot(send_hit.astype(jnp.bfloat16), queries, preferred_element_type=jnp.float32).astype(jnp.bfloat16)
    q_pos = jnp.sum(jnp.where(send_hit, here[None, :], 0), axis=1)
    q_seg = jnp.sum(jnp.where(send_hit, q_seg[None, :], 0), axis=1)
    carry = attention(q_sent, [row], q_pos, q_seg, k_pos[2:], k_seg[2:], scale, final=False)
    fetched, carry = lax.optimization_barrier((fetched, carry))
    swapped = lax.ppermute(fetched, "core", perm=[(i, (i + 1) % n_core) for i in range(n_core)])
    to_send = attention(
        q_sent, [fetched, swapped], q_pos, q_seg, k_pos[:2], k_seg[:2], scale, carry=carry
    )

    width = to_send.shape[1]
    by_dest = jnp.transpose(to_send.reshape(n_y, n_x, chunk, width), (1, 0, 2, 3))
    over_x = lax.all_to_all(by_dest, "x", split_axis=0, concat_axis=0, tiled=True)
    over_x = jnp.transpose(over_x, (1, 0, 2, 3))
    arrived = lax.all_to_all(over_x, "y", split_axis=0, concat_axis=0, tiled=True)
    arrived = arrived.reshape(rows, width)

    src = lax.dynamic_slice_in_dim(relayout, s * rows, rows, 0) // rows
    before = jnp.arange(rows)[None, :] < jnp.arange(rows)[:, None]
    nth = jnp.sum((before & (src[None, :] == src[:, None])).astype(jnp.int32), axis=1)
    slot = src * chunk + nth
    per_dev = rows // (n_z * n_core)
    slot3 = slot.reshape(n_z, n_core, per_dev)
    cols = jnp.arange(rows, dtype=jnp.int32)[None, :]

    def project(which):
        chosen = jnp.take(slot3, which, axis=1).reshape(-1)
        sel = (chosen[:, None] == cols).astype(jnp.bfloat16)
        relaid = jnp.dot(sel, arrived, preferred_element_type=jnp.float32).astype(jnp.bfloat16)
        return jnp.dot(relaid, out_weight, preferred_element_type=jnp.float32).astype(jnp.bfloat16)

    part_other = project(n_core - 1 - c)
    got = lax.ppermute(part_other, "core", perm=[(0, 1), (1, 0)])
    part_own = lax.optimization_barrier(project(c))
    half = (part_own.astype(jnp.float32) + got.astype(jnp.float32)).astype(jnp.bfloat16)
    return lax.psum_scatter(half, "z", scatter_dimension=0, tiled=True)

def solution(mesh):
    n_seq, n_tp = mesh.devices.shape
    n_x = 4
    mesh4 = Mesh(mesh.devices.reshape(n_seq // n_x, n_x, n_tp // 2, 2), ("y", "x", "z", "core"))
    seq = ("y", "x")
    tp = ("z", "core")
    return jax.shard_map(
        shards,
        mesh=mesh4,
        in_specs=(
            P(),
            P(),
            P(seq, tp),
            P(seq + tp, None),
            P(seq + tp, None),
            P(tp, None),
        ),
        out_specs=P(seq + tp, None),
        check_vma=False,
    )
```

```python
import functools

import jax
import jax.numpy as jnp
import numpy as np
from jax import lax
from jax.experimental import pallas as pl
from jax.sharding import Mesh
from jax.sharding import PartitionSpec as P

QH = 32
KVH = 4
HD = 128
MOST_LEN = 2048


def _attention_body(scale, n_pieces, heads, carry_in, final, q_ref, *refs):
    kv_refs = refs[:n_pieces]
    refs = refs[n_pieces:]
    qp_ref, qs_ref, kp_ref, ks_ref = refs[:4]
    refs = refs[4:]
    if carry_in:
        m_in, l_in, acc_in = refs[:3]
        refs = refs[3:]
    qp = qp_ref[...]
    qs = qs_ref[...]
    lives = [(kp_ref[pl.ds(p, 1), :] <= qp) & (ks_ref[pl.ds(p, 1), :] == qs) for p in range(n_pieces)]
    for h in range(heads):
        q = q_ref[:, pl.ds(h * HD, HD)]
        scores = [
            jnp.where(
                lives[p],
                lax.dot_general(
                    q, kv_refs[p][:, pl.ds(0, HD)], (((1,), (1,)), ((), ())),
                    preferred_element_type=jnp.float32,
                ) * scale,
                jnp.float32(-1e30),
            )
            for p in range(n_pieces)
        ]
        peak = functools.reduce(jnp.maximum, [jnp.max(s, axis=1, keepdims=True) for s in scores])
        if carry_in:
            peak = jnp.maximum(peak, m_in[h])
        expos = [jnp.where(lives[p], jnp.exp(scores[p] - peak), jnp.float32(0.0)) for p in range(n_pieces)]
        denom = functools.reduce(jnp.add, [jnp.sum(e, axis=1, keepdims=True) for e in expos])
        summed = functools.reduce(
            jnp.add,
            [
                jnp.dot(expos[p].astype(jnp.bfloat16), kv_refs[p][:, pl.ds(HD, HD)], preferred_element_type=jnp.float32)
                for p in range(n_pieces)
            ],
        )
        if carry_in:
            alpha = jnp.exp(m_in[h] - peak)
            denom = denom + alpha * l_in[h]
            summed = summed + alpha * acc_in[:, pl.ds(h * HD, HD)]
        if final:
            refs[0][:, pl.ds(h * HD, HD)] = (summed / denom).astype(refs[0].dtype)
        else:
            refs[0][h] = peak
            refs[1][h] = denom
            refs[2][:, pl.ds(h * HD, HD)] = summed


def attention(q, pieces, q_pos, q_seg, k_pos, k_seg, scale, carry=None, final=True):
    rows, width = q.shape
    heads = width // HD
    n_pieces = len(pieces)
    n = pieces[0].shape[0]
    args = [q, *pieces, q_pos.reshape(rows, 1), q_seg.reshape(rows, 1), k_pos, k_seg]
    if carry is not None:
        args += list(carry)
    if final:
        out_shape = jax.ShapeDtypeStruct((rows, width), jnp.bfloat16)
    else:
        out_shape = [
            jax.ShapeDtypeStruct((heads, rows, 1), jnp.float32),
            jax.ShapeDtypeStruct((heads, rows, 1), jnp.float32),
            jax.ShapeDtypeStruct((rows, width), jnp.float32),
        ]
    return pl.pallas_call(
        functools.partial(_attention_body, scale, n_pieces, heads, carry is not None, final),
        out_shape=out_shape,
        cost_estimate=pl.CostEstimate(
            flops=4 * rows * n * n_pieces * HD * heads,
            transcendentals=rows * n * n_pieces * heads,
            bytes_accessed=2 * (2 * rows * width + 2 * n_pieces * n * HD),
        ),
    )(*args)


def shards(segment_ids, relayout, queries, keys, values, out_weight):
    rows = queries.shape[0]
    n_seq = lax.axis_size("y") * lax.axis_size("x")
    n_z = lax.axis_size("z")
    n_core = lax.axis_size("core")
    s = lax.axis_index("y") * lax.axis_size("x") + lax.axis_index("x")
    t = lax.axis_index("z") * n_core + lax.axis_index("core")
    heads_here = queries.shape[1] // HD
    group = QH // KVH
    kv_width = keys.shape[1]
    scale = HD ** (-0.5)
    back = -(-(MOST_LEN - 1) // rows)
    back = min(back, n_seq - 1)

    n_tp = n_z * n_core
    kv_heads = kv_width // HD
    n_x = lax.axis_size("x")
    share = group // heads_here
    assert n_tp == kv_heads * share
    k_h = jnp.transpose(keys.reshape(keys.shape[0], kv_heads, HD), (1, 0, 2))
    v_h = jnp.transpose(values.reshape(values.shape[0], kv_heads, HD), (1, 0, 2))
    kv_h = jnp.concatenate([k_h, v_h], axis=2)
    pieces = jnp.broadcast_to(
        kv_h[None, :, None], (n_x, kv_heads, share) + kv_h.shape[1:]
    ).reshape((n_x * n_tp,) + kv_h.shape[1:])
    row = lax.all_to_all(pieces, ("x", "z", "core"), split_axis=0, concat_axis=0, tiled=True)
    row = row.reshape(n_x * rows, 2 * HD)

    n_y = lax.axis_size("y")
    x = lax.axis_index("x")
    c = lax.axis_index("core")
    rows_back = -(-back // n_x)
    assert rows_back == n_core
    perm = []
    for cc in range(n_core):
        k = cc + 1
        if k <= rows_back:
            perm += [(yy * n_core + cc, (yy + k) * n_core + cc) for yy in range(n_y - k)]
    fetched = lax.ppermute(row, ("y", "core"), perm=perm)
    y = lax.axis_index("y")
    span = n_x * rows
    piece_rows = [y - 1 - c, y - n_core + c, y]
    k_pos = jnp.stack([r * span + jnp.arange(span, dtype=jnp.int32) for r in piece_rows])
    pad = rows_back * span
    seg_pad = jnp.concatenate([jnp.full((pad,), -1, jnp.int32), segment_ids])
    k_seg = jnp.stack([lax.dynamic_slice_in_dim(seg_pad, r * span + pad, span, 0) for r in piece_rows])
    q_pos = s * rows + jnp.arange(rows, dtype=jnp.int32)
    q_seg = lax.dynamic_slice_in_dim(segment_ids, s * rows, rows, 0)
    chunk = rows // n_seq
    total = relayout.shape[0]
    here = s * rows + jnp.arange(rows, dtype=jnp.int32)
    new_of = jnp.sum(
        jnp.where(relayout[None, :] == here[:, None], jnp.arange(total, dtype=jnp.int32)[None, :], 0),
        axis=1,
    )
    rank = jnp.sum((new_of[None, :] < new_of[:, None]).astype(jnp.int32), axis=1)
    send_hit = rank[None, :] == jnp.arange(rows, dtype=jnp.int32)[:, None]
    q_sent = jnp.dot(send_hit.astype(jnp.bfloat16), queries, preferred_element_type=jnp.float32).astype(jnp.bfloat16)
    q_pos = jnp.sum(jnp.where(send_hit, here[None, :], 0), axis=1)
    q_seg = jnp.sum(jnp.where(send_hit, q_seg[None, :], 0), axis=1)
    carry = attention(q_sent, [row], q_pos, q_seg, k_pos[2:], k_seg[2:], scale, final=False)
    fetched, carry = lax.optimization_barrier((fetched, carry))
    swapped = lax.ppermute(fetched, "core", perm=[(i, (i + 1) % n_core) for i in range(n_core)])
    to_send = attention(
        q_sent, [fetched, swapped], q_pos, q_seg, k_pos[:2], k_seg[:2], scale, carry=carry
    )

    arrived = lax.all_to_all(to_send, ("y", "x"), split_axis=0, concat_axis=0, tiled=True)

    src = lax.dynamic_slice_in_dim(relayout, s * rows, rows, 0) // rows
    before = jnp.arange(rows)[None, :] < jnp.arange(rows)[:, None]
    nth = jnp.sum((before & (src[None, :] == src[:, None])).astype(jnp.int32), axis=1)
    slot = src * chunk + nth
    per_dev = rows // (n_z * n_core)
    slot3 = slot.reshape(n_z, n_core, per_dev)
    cols = jnp.arange(rows, dtype=jnp.int32)[None, :]

    def project(which):
        chosen = jnp.take(slot3, which, axis=1).reshape(-1)
        sel = (chosen[:, None] == cols).astype(jnp.bfloat16)
        relaid = jnp.dot(sel, arrived, preferred_element_type=jnp.float32).astype(jnp.bfloat16)
        return jnp.dot(relaid, out_weight, preferred_element_type=jnp.float32).astype(jnp.bfloat16)

    part_other = project(n_core - 1 - c)
    got = lax.ppermute(part_other, "core", perm=[(0, 1), (1, 0)])
    part_own = lax.optimization_barrier(project(c))
    half = (part_own.astype(jnp.float32) + got.astype(jnp.float32)).astype(jnp.bfloat16)
    return lax.psum_scatter(half, "z", scatter_dimension=0, tiled=True)

def solution(mesh):
    n_seq, n_tp = mesh.devices.shape
    n_x = 4
    mesh4 = Mesh(mesh.devices.reshape(n_seq // n_x, n_x, n_tp // 2, 2), ("y", "x", "z", "core"))
    seq = ("y", "x")
    tp = ("z", "core")
    return jax.shard_map(
        shards,
        mesh=mesh4,
        in_specs=(
            P(),
            P(),
            P(seq, tp),
            P(seq + tp, None),
            P(seq + tp, None),
            P(tp, None),
        ),
        out_specs=P(seq + tp, None),
        check_vma=False,
    )
```

```python
import functools

import jax
import jax.numpy as jnp
import numpy as np
from jax import lax
from jax.experimental import pallas as pl
from jax.sharding import Mesh
from jax.sharding import PartitionSpec as P

QH = 32
KVH = 4
HD = 128
MOST_LEN = 2048


def _attention_body(scale, n_pieces, heads, carry_in, final, q_ref, *refs):
    kv_refs = refs[:n_pieces]
    refs = refs[n_pieces:]
    qp_ref, qs_ref, kp_ref, ks_ref = refs[:4]
    refs = refs[4:]
    if carry_in:
        m_in, l_in, acc_in = refs[:3]
        refs = refs[3:]
    qp = qp_ref[...]
    qs = qs_ref[...]
    lives = [(kp_ref[pl.ds(p, 1), :] <= qp) & (ks_ref[pl.ds(p, 1), :] == qs) for p in range(n_pieces)]
    for h in range(heads):
        q = q_ref[:, pl.ds(h * HD, HD)]
        scores = [
            jnp.where(
                lives[p],
                lax.dot_general(
                    q, kv_refs[p][:, pl.ds(0, HD)], (((1,), (1,)), ((), ())),
                    preferred_element_type=jnp.float32,
                ) * scale,
                jnp.float32(-1e30),
            )
            for p in range(n_pieces)
        ]
        peak = functools.reduce(jnp.maximum, [jnp.max(s, axis=1, keepdims=True) for s in scores])
        if carry_in:
            peak = jnp.maximum(peak, m_in[h])
        expos = [jnp.where(lives[p], jnp.exp(scores[p] - peak), jnp.float32(0.0)) for p in range(n_pieces)]
        denom = functools.reduce(jnp.add, [jnp.sum(e, axis=1, keepdims=True) for e in expos])
        summed = functools.reduce(
            jnp.add,
            [
                jnp.dot(expos[p].astype(jnp.bfloat16), kv_refs[p][:, pl.ds(HD, HD)], preferred_element_type=jnp.float32)
                for p in range(n_pieces)
            ],
        )
        if carry_in:
            alpha = jnp.exp(m_in[h] - peak)
            denom = denom + alpha * l_in[h]
            summed = summed + alpha * acc_in[:, pl.ds(h * HD, HD)]
        if final:
            refs[0][:, pl.ds(h * HD, HD)] = (summed / denom).astype(refs[0].dtype)
        else:
            refs[0][h] = peak
            refs[1][h] = denom
            refs[2][:, pl.ds(h * HD, HD)] = summed


def attention(q, pieces, q_pos, q_seg, k_pos, k_seg, scale, carry=None, final=True):
    rows, width = q.shape
    heads = width // HD
    n_pieces = len(pieces)
    n = pieces[0].shape[0]
    args = [q, *pieces, q_pos.reshape(rows, 1), q_seg.reshape(rows, 1), k_pos, k_seg]
    if carry is not None:
        args += list(carry)
    if final:
        out_shape = jax.ShapeDtypeStruct((rows, width), jnp.bfloat16)
    else:
        out_shape = [
            jax.ShapeDtypeStruct((heads, rows, 1), jnp.float32),
            jax.ShapeDtypeStruct((heads, rows, 1), jnp.float32),
            jax.ShapeDtypeStruct((rows, width), jnp.float32),
        ]
    return pl.pallas_call(
        functools.partial(_attention_body, scale, n_pieces, heads, carry is not None, final),
        out_shape=out_shape,
        cost_estimate=pl.CostEstimate(
            flops=4 * rows * n * n_pieces * HD * heads,
            transcendentals=rows * n * n_pieces * heads,
            bytes_accessed=2 * (2 * rows * width + 2 * n_pieces * n * HD),
        ),
    )(*args)


def shards(segment_ids, relayout, queries, keys, values, out_weight):
    rows = queries.shape[0]
    n_seq = lax.axis_size("y") * lax.axis_size("x")
    n_z = lax.axis_size("z")
    n_core = lax.axis_size("core")
    s = lax.axis_index("y") * lax.axis_size("x") + lax.axis_index("x")
    t = lax.axis_index("z") * n_core + lax.axis_index("core")
    heads_here = queries.shape[1] // HD
    group = QH // KVH
    kv_width = keys.shape[1]
    scale = HD ** (-0.5)
    back = -(-(MOST_LEN - 1) // rows)
    back = min(back, n_seq - 1)

    n_tp = n_z * n_core
    kv_heads = kv_width // HD
    n_x = lax.axis_size("x")
    share = group // heads_here
    assert n_tp == kv_heads * share
    k_h = jnp.transpose(keys.reshape(keys.shape[0], kv_heads, HD), (1, 0, 2))
    v_h = jnp.transpose(values.reshape(values.shape[0], kv_heads, HD), (1, 0, 2))
    kv_h = jnp.concatenate([k_h, v_h], axis=2)
    pieces = jnp.broadcast_to(
        kv_h[None, :, None], (n_x, kv_heads, share) + kv_h.shape[1:]
    ).reshape((n_x * n_tp,) + kv_h.shape[1:])
    row = lax.all_to_all(pieces, ("x", "z", "core"), split_axis=0, concat_axis=0, tiled=True)
    row = row.reshape(n_x * rows, 2 * HD)

    n_y = lax.axis_size("y")
    x = lax.axis_index("x")
    c = lax.axis_index("core")
    rows_back = -(-back // n_x)
    assert rows_back == n_core
    perm = []
    for cc in range(n_core):
        k = cc + 1
        if k <= rows_back:
            perm += [(yy * n_core + cc, (yy + k) * n_core + cc) for yy in range(n_y - k)]
    fetched = lax.ppermute(row, ("y", "core"), perm=perm)
    y = lax.axis_index("y")
    span = n_x * rows
    piece_rows = [y - 1 - c, y - n_core + c, y]
    k_pos = jnp.stack([r * span + jnp.arange(span, dtype=jnp.int32) for r in piece_rows])
    pad = rows_back * span
    seg_pad = jnp.concatenate([jnp.full((pad,), -1, jnp.int32), segment_ids])
    k_seg = jnp.stack([lax.dynamic_slice_in_dim(seg_pad, r * span + pad, span, 0) for r in piece_rows])
    q_pos = s * rows + jnp.arange(rows, dtype=jnp.int32)
    q_seg = lax.dynamic_slice_in_dim(segment_ids, s * rows, rows, 0)
    chunk = rows // n_seq
    total = relayout.shape[0]
    here = s * rows + jnp.arange(rows, dtype=jnp.int32)
    new_of = jnp.sum(
        jnp.where(relayout[None, :] == here[:, None], jnp.arange(total, dtype=jnp.int32)[None, :], 0),
        axis=1,
    )
    rank = jnp.sum((new_of[None, :] < new_of[:, None]).astype(jnp.int32), axis=1)
    send_hit = rank[None, :] == jnp.arange(rows, dtype=jnp.int32)[:, None]
    q_sent = jnp.dot(send_hit.astype(jnp.bfloat16), queries, preferred_element_type=jnp.float32).astype(jnp.bfloat16)
    q_pos = jnp.sum(jnp.where(send_hit, here[None, :], 0), axis=1)
    q_seg = jnp.sum(jnp.where(send_hit, q_seg[None, :], 0), axis=1)
    carry = attention(q_sent, [row], q_pos, q_seg, k_pos[2:], k_seg[2:], scale, final=False)
    src = lax.dynamic_slice_in_dim(relayout, s * rows, rows, 0) // rows
    before = jnp.arange(rows)[None, :] < jnp.arange(rows)[:, None]
    nth = jnp.sum((before & (src[None, :] == src[:, None])).astype(jnp.int32), axis=1)
    slot = src * chunk + nth
    fetched, carry, kp_early, ks_early, slot = lax.optimization_barrier(
        (fetched, carry, k_pos[:2], k_seg[:2], slot)
    )
    swapped = lax.ppermute(fetched, "core", perm=[(i, (i + 1) % n_core) for i in range(n_core)])
    to_send = attention(
        q_sent, [fetched, swapped], q_pos, q_seg, kp_early, ks_early, scale, carry=carry
    )

    arrived = lax.all_to_all(to_send, ("y", "x"), split_axis=0, concat_axis=0, tiled=True)

    per_dev = rows // (n_z * n_core)
    slot3 = slot.reshape(n_z, n_core, per_dev)
    cols = jnp.arange(rows, dtype=jnp.int32)[None, :]

    def project(which):
        chosen = jnp.take(slot3, which, axis=1).reshape(-1)
        sel = (chosen[:, None] == cols).astype(jnp.bfloat16)
        relaid = jnp.dot(sel, arrived, preferred_element_type=jnp.float32).astype(jnp.bfloat16)
        return jnp.dot(relaid, out_weight, preferred_element_type=jnp.float32).astype(jnp.bfloat16)

    part_other = project(n_core - 1 - c)
    got = lax.ppermute(part_other, "core", perm=[(0, 1), (1, 0)])
    part_own = lax.optimization_barrier(project(c))
    half = (part_own.astype(jnp.float32) + got.astype(jnp.float32)).astype(jnp.bfloat16)
    return lax.psum_scatter(half, "z", scatter_dimension=0, tiled=True)

def solution(mesh):
    n_seq, n_tp = mesh.devices.shape
    n_x = 4
    mesh4 = Mesh(mesh.devices.reshape(n_seq // n_x, n_x, n_tp // 2, 2), ("y", "x", "z", "core"))
    seq = ("y", "x")
    tp = ("z", "core")
    return jax.shard_map(
        shards,
        mesh=mesh4,
        in_specs=(
            P(),
            P(),
            P(seq, tp),
            P(seq + tp, None),
            P(seq + tp, None),
            P(tp, None),
        ),
        out_specs=P(seq + tp, None),
        check_vma=False,
    )
```

```python
import functools

import jax
import jax.numpy as jnp
import numpy as np
from jax import lax
from jax.experimental import pallas as pl
from jax.sharding import Mesh
from jax.sharding import PartitionSpec as P

QH = 32
KVH = 4
HD = 128
MOST_LEN = 2048


def _attention_body(scale, n_pieces, heads, carry_in, final, q_ref, *refs):
    kv_refs = refs[:n_pieces]
    refs = refs[n_pieces:]
    qp_ref, qs_ref, kp_ref, ks_ref = refs[:4]
    refs = refs[4:]
    if carry_in:
        m_in, l_in, acc_in = refs[:3]
        refs = refs[3:]
    qp = qp_ref[...]
    qs = qs_ref[...]
    lives = [(kp_ref[pl.ds(p, 1), :] <= qp) & (ks_ref[pl.ds(p, 1), :] == qs) for p in range(n_pieces)]
    for h in range(heads):
        q = q_ref[:, pl.ds(h * HD, HD)]
        scores = [
            jnp.where(
                lives[p],
                lax.dot_general(
                    q, kv_refs[p][:, pl.ds(0, HD)], (((1,), (1,)), ((), ())),
                    preferred_element_type=jnp.float32,
                ) * scale,
                jnp.float32(-1e30),
            )
            for p in range(n_pieces)
        ]
        peak = functools.reduce(jnp.maximum, [jnp.max(s, axis=1, keepdims=True) for s in scores])
        if carry_in:
            peak = jnp.maximum(peak, m_in[h])
        expos = [jnp.where(lives[p], jnp.exp(scores[p] - peak), jnp.float32(0.0)) for p in range(n_pieces)]
        denom = functools.reduce(jnp.add, [jnp.sum(e, axis=1, keepdims=True) for e in expos])
        summed = functools.reduce(
            jnp.add,
            [
                jnp.dot(expos[p].astype(jnp.bfloat16), kv_refs[p][:, pl.ds(HD, HD)], preferred_element_type=jnp.float32)
                for p in range(n_pieces)
            ],
        )
        if carry_in:
            alpha = jnp.exp(m_in[h] - peak)
            denom = denom + alpha * l_in[h]
            summed = summed + alpha * acc_in[:, pl.ds(h * HD, HD)]
        if final:
            refs[0][:, pl.ds(h * HD, HD)] = (summed / denom).astype(refs[0].dtype)
        else:
            refs[0][h] = peak
            refs[1][h] = denom
            refs[2][:, pl.ds(h * HD, HD)] = summed


def attention(q, pieces, q_pos, q_seg, k_pos, k_seg, scale, carry=None, final=True):
    rows, width = q.shape
    heads = width // HD
    n_pieces = len(pieces)
    n = pieces[0].shape[0]
    args = [q, *pieces, q_pos.reshape(rows, 1), q_seg.reshape(rows, 1), k_pos, k_seg]
    if carry is not None:
        args += list(carry)
    if final:
        out_shape = jax.ShapeDtypeStruct((rows, width), jnp.bfloat16)
    else:
        out_shape = [
            jax.ShapeDtypeStruct((heads, rows, 1), jnp.float32),
            jax.ShapeDtypeStruct((heads, rows, 1), jnp.float32),
            jax.ShapeDtypeStruct((rows, width), jnp.float32),
        ]
    return pl.pallas_call(
        functools.partial(_attention_body, scale, n_pieces, heads, carry is not None, final),
        out_shape=out_shape,
        cost_estimate=pl.CostEstimate(
            flops=4 * rows * n * n_pieces * HD * heads,
            transcendentals=rows * n * n_pieces * heads,
            bytes_accessed=2 * (2 * rows * width + 2 * n_pieces * n * HD),
        ),
    )(*args)


def shards(segment_ids, relayout, queries, keys, values, out_weight):
    rows = queries.shape[0]
    n_seq = lax.axis_size("y") * lax.axis_size("x")
    n_z = lax.axis_size("z")
    n_core = lax.axis_size("core")
    s = lax.axis_index("y") * lax.axis_size("x") + lax.axis_index("x")
    t = lax.axis_index("z") * n_core + lax.axis_index("core")
    heads_here = queries.shape[1] // HD
    group = QH // KVH
    kv_width = keys.shape[1]
    scale = HD ** (-0.5)
    back = -(-(MOST_LEN - 1) // rows)
    back = min(back, n_seq - 1)

    n_tp = n_z * n_core
    kv_heads = kv_width // HD
    n_x = lax.axis_size("x")
    share = group // heads_here
    assert n_tp == kv_heads * share
    k_h = jnp.transpose(keys.reshape(keys.shape[0], kv_heads, HD), (1, 0, 2))
    v_h = jnp.transpose(values.reshape(values.shape[0], kv_heads, HD), (1, 0, 2))
    kv_h = jnp.concatenate([k_h, v_h], axis=2)
    pieces = jnp.broadcast_to(
        kv_h[None, :, None], (n_x, kv_heads, share) + kv_h.shape[1:]
    ).reshape((n_x * n_tp,) + kv_h.shape[1:])
    row = lax.all_to_all(pieces, ("x", "z", "core"), split_axis=0, concat_axis=0, tiled=True)
    row = row.reshape(n_x * rows, 2 * HD)

    n_y = lax.axis_size("y")
    x = lax.axis_index("x")
    c = lax.axis_index("core")
    rows_back = -(-back // n_x)
    assert rows_back == n_core
    perm = []
    for cc in range(n_core):
        k = cc + 1
        if k <= rows_back:
            perm += [(yy * n_core + cc, (yy + k) * n_core + cc) for yy in range(n_y - k)]
    fetched = lax.ppermute(row, ("y", "core"), perm=perm)
    y = lax.axis_index("y")
    span = n_x * rows
    piece_rows = [y - 1 - c, y - n_core + c, y]
    k_pos = jnp.stack([r * span + jnp.arange(span, dtype=jnp.int32) for r in piece_rows])
    pad = rows_back * span
    seg_pad = jnp.concatenate([jnp.full((pad,), -1, jnp.int32), segment_ids])
    k_seg = jnp.stack([lax.dynamic_slice_in_dim(seg_pad, r * span + pad, span, 0) for r in piece_rows])
    q_pos = s * rows + jnp.arange(rows, dtype=jnp.int32)
    q_seg = lax.dynamic_slice_in_dim(segment_ids, s * rows, rows, 0)
    chunk = rows // n_seq
    total = relayout.shape[0]
    here = s * rows + jnp.arange(rows, dtype=jnp.int32)
    new_of = jnp.sum(
        jnp.where(relayout[None, :] == here[:, None], jnp.arange(total, dtype=jnp.int32)[None, :], 0),
        axis=1,
    )
    rank = jnp.sum((new_of[None, :] < new_of[:, None]).astype(jnp.int32), axis=1)
    send_hit = rank[None, :] == jnp.arange(rows, dtype=jnp.int32)[:, None]
    q_sent = jnp.dot(send_hit.astype(jnp.bfloat16), queries, preferred_element_type=jnp.float32).astype(jnp.bfloat16)
    q_pos = jnp.sum(jnp.where(send_hit, here[None, :], 0), axis=1)
    q_seg = jnp.sum(jnp.where(send_hit, q_seg[None, :], 0), axis=1)
    carry = attention(q_sent, [row], q_pos, q_seg, k_pos[2:], k_seg[2:], scale, final=False)
    src = lax.dynamic_slice_in_dim(relayout, s * rows, rows, 0) // rows
    before = jnp.arange(rows)[None, :] < jnp.arange(rows)[:, None]
    nth = jnp.sum((before & (src[None, :] == src[:, None])).astype(jnp.int32), axis=1)
    slot = src * chunk + nth
    fetched, carry, kp_early, ks_early, slot = lax.optimization_barrier(
        (fetched, carry, k_pos[:2], k_seg[:2], slot)
    )
    swapped = lax.ppermute(fetched, "core", perm=[(i, (i + 1) % n_core) for i in range(n_core)])
    carry = attention(
        q_sent, [fetched], q_pos, q_seg, kp_early[:1], ks_early[:1], scale, carry=carry, final=False
    )
    to_send = attention(
        q_sent, [swapped], q_pos, q_seg, kp_early[1:], ks_early[1:], scale, carry=carry
    )

    arrived = lax.all_to_all(to_send, ("y", "x"), split_axis=0, concat_axis=0, tiled=True)

    per_dev = rows // (n_z * n_core)
    slot3 = slot.reshape(n_z, n_core, per_dev)
    cols = jnp.arange(rows, dtype=jnp.int32)[None, :]

    def project(which):
        chosen = jnp.take(slot3, which, axis=1).reshape(-1)
        sel = (chosen[:, None] == cols).astype(jnp.bfloat16)
        relaid = jnp.dot(sel, arrived, preferred_element_type=jnp.float32).astype(jnp.bfloat16)
        return jnp.dot(relaid, out_weight, preferred_element_type=jnp.float32).astype(jnp.bfloat16)

    part_other = project(n_core - 1 - c)
    got = lax.ppermute(part_other, "core", perm=[(0, 1), (1, 0)])
    part_own = lax.optimization_barrier(project(c))
    half = (part_own.astype(jnp.float32) + got.astype(jnp.float32)).astype(jnp.bfloat16)
    return lax.psum_scatter(half, "z", scatter_dimension=0, tiled=True)

def solution(mesh):
    n_seq, n_tp = mesh.devices.shape
    n_x = 4
    mesh4 = Mesh(mesh.devices.reshape(n_seq // n_x, n_x, n_tp // 2, 2), ("y", "x", "z", "core"))
    seq = ("y", "x")
    tp = ("z", "core")
    return jax.shard_map(
        shards,
        mesh=mesh4,
        in_specs=(
            P(),
            P(),
            P(seq, tp),
            P(seq + tp, None),
            P(seq + tp, None),
            P(tp, None),
        ),
        out_specs=P(seq + tp, None),
        check_vma=False,
    )
```

```python
import functools

import jax
import jax.numpy as jnp
import numpy as np
from jax import lax
from jax.experimental import pallas as pl
from jax.sharding import Mesh
from jax.sharding import PartitionSpec as P

QH = 32
KVH = 4
HD = 128
MOST_LEN = 2048


def _attention_body(scale, n_pieces, heads, carry_in, final, q_ref, *refs):
    kv_refs = refs[:n_pieces]
    refs = refs[n_pieces:]
    qp_ref, qs_ref, kp_ref, ks_ref = refs[:4]
    refs = refs[4:]
    if carry_in:
        m_in, l_in, acc_in = refs[:3]
        refs = refs[3:]
    qp = qp_ref[...]
    qs = qs_ref[...]
    lives = [(kp_ref[pl.ds(p, 1), :] <= qp) & (ks_ref[pl.ds(p, 1), :] == qs) for p in range(n_pieces)]
    for h in range(heads):
        q = q_ref[:, pl.ds(h * HD, HD)]
        scores = [
            jnp.where(
                lives[p],
                lax.dot_general(
                    q, kv_refs[p][:, pl.ds(0, HD)], (((1,), (1,)), ((), ())),
                    preferred_element_type=jnp.float32,
                ) * scale,
                jnp.float32(-1e30),
            )
            for p in range(n_pieces)
        ]
        peak = functools.reduce(jnp.maximum, [jnp.max(s, axis=1, keepdims=True) for s in scores])
        if carry_in:
            peak = jnp.maximum(peak, m_in[h])
        expos = [jnp.where(lives[p], jnp.exp(scores[p] - peak), jnp.float32(0.0)) for p in range(n_pieces)]
        denom = functools.reduce(jnp.add, [jnp.sum(e, axis=1, keepdims=True) for e in expos])
        summed = functools.reduce(
            jnp.add,
            [
                jnp.dot(expos[p].astype(jnp.bfloat16), kv_refs[p][:, pl.ds(HD, HD)], preferred_element_type=jnp.float32)
                for p in range(n_pieces)
            ],
        )
        if carry_in:
            alpha = jnp.exp(m_in[h] - peak)
            denom = denom + alpha * l_in[h]
            summed = summed + alpha * acc_in[:, pl.ds(h * HD, HD)]
        if final:
            refs[0][:, pl.ds(h * HD, HD)] = (summed / denom).astype(refs[0].dtype)
        else:
            refs[0][h] = peak
            refs[1][h] = denom
            refs[2][:, pl.ds(h * HD, HD)] = summed


def attention(q, pieces, q_pos, q_seg, k_pos, k_seg, scale, carry=None, final=True):
    rows, width = q.shape
    heads = width // HD
    n_pieces = len(pieces)
    n = pieces[0].shape[0]
    args = [q, *pieces, q_pos.reshape(rows, 1), q_seg.reshape(rows, 1), k_pos, k_seg]
    if carry is not None:
        args += list(carry)
    if final:
        out_shape = jax.ShapeDtypeStruct((rows, width), jnp.bfloat16)
    else:
        out_shape = [
            jax.ShapeDtypeStruct((heads, rows, 1), jnp.float32),
            jax.ShapeDtypeStruct((heads, rows, 1), jnp.float32),
            jax.ShapeDtypeStruct((rows, width), jnp.float32),
        ]
    return pl.pallas_call(
        functools.partial(_attention_body, scale, n_pieces, heads, carry is not None, final),
        out_shape=out_shape,
        cost_estimate=pl.CostEstimate(
            flops=4 * rows * n * n_pieces * HD * heads,
            transcendentals=rows * n * n_pieces * heads,
            bytes_accessed=2 * (2 * rows * width + 2 * n_pieces * n * HD),
        ),
    )(*args)


def shards(segment_ids, relayout, queries, keys, values, out_weight):
    rows = queries.shape[0]
    n_seq = lax.axis_size("y") * lax.axis_size("x")
    n_z = lax.axis_size("z")
    n_core = lax.axis_size("core")
    s = lax.axis_index("y") * lax.axis_size("x") + lax.axis_index("x")
    t = lax.axis_index("z") * n_core + lax.axis_index("core")
    heads_here = queries.shape[1] // HD
    group = QH // KVH
    kv_width = keys.shape[1]
    scale = HD ** (-0.5)
    back = -(-(MOST_LEN - 1) // rows)
    back = min(back, n_seq - 1)

    n_tp = n_z * n_core
    kv_heads = kv_width // HD
    n_x = lax.axis_size("x")
    share = group // heads_here
    assert n_tp == kv_heads * share
    k_h = jnp.transpose(keys.reshape(keys.shape[0], kv_heads, HD), (1, 0, 2))
    v_h = jnp.transpose(values.reshape(values.shape[0], kv_heads, HD), (1, 0, 2))
    kv_h = jnp.concatenate([k_h, v_h], axis=2)
    pieces = jnp.broadcast_to(
        kv_h[None, :, None], (n_x, kv_heads, share) + kv_h.shape[1:]
    ).reshape((n_x * n_tp,) + kv_h.shape[1:])
    row = lax.all_to_all(pieces, ("x", "z", "core"), split_axis=0, concat_axis=0, tiled=True)
    row = row.reshape(n_x * rows, 2 * HD)

    n_y = lax.axis_size("y")
    x = lax.axis_index("x")
    c = lax.axis_index("core")
    rows_back = -(-back // n_x)
    assert rows_back == n_core
    perm = []
    for cc in range(n_core):
        k = cc + 1
        if k <= rows_back:
            perm += [(yy * n_core + cc, (yy + k) * n_core + cc) for yy in range(n_y - k)]
    fetched = lax.ppermute(row, ("y", "core"), perm=perm)
    y = lax.axis_index("y")
    span = n_x * rows
    piece_rows = [y - 1 - c, y - n_core + c, y]
    k_pos = jnp.stack([r * span + jnp.arange(span, dtype=jnp.int32) for r in piece_rows])
    pad = rows_back * span
    seg_pad = jnp.concatenate([jnp.full((pad,), -1, jnp.int32), segment_ids])
    k_seg = jnp.stack([lax.dynamic_slice_in_dim(seg_pad, r * span + pad, span, 0) for r in piece_rows])
    q_pos = s * rows + jnp.arange(rows, dtype=jnp.int32)
    q_seg = lax.dynamic_slice_in_dim(segment_ids, s * rows, rows, 0)
    chunk = rows // n_seq
    total = relayout.shape[0]
    here = s * rows + jnp.arange(rows, dtype=jnp.int32)
    new_of = jnp.sum(
        jnp.where(relayout[None, :] == here[:, None], jnp.arange(total, dtype=jnp.int32)[None, :], 0),
        axis=1,
    )
    rank = jnp.sum((new_of[None, :] < new_of[:, None]).astype(jnp.int32), axis=1)
    send_hit = rank[None, :] == jnp.arange(rows, dtype=jnp.int32)[:, None]
    q_sent = jnp.dot(send_hit.astype(jnp.bfloat16), queries, preferred_element_type=jnp.float32).astype(jnp.bfloat16)
    q_pos = jnp.sum(jnp.where(send_hit, here[None, :], 0), axis=1)
    q_seg = jnp.sum(jnp.where(send_hit, q_seg[None, :], 0), axis=1)
    carry = attention(q_sent, [row], q_pos, q_seg, k_pos[2:], k_seg[2:], scale, final=False)
    fetched, carry = lax.optimization_barrier((fetched, carry))
    swapped = lax.ppermute(fetched, "core", perm=[(i, (i + 1) % n_core) for i in range(n_core)])
    to_send = attention(
        q_sent, [fetched, swapped], q_pos, q_seg, k_pos[:2], k_seg[:2], scale, carry=carry
    )

    arrived = lax.all_to_all(to_send, ("y", "x"), split_axis=0, concat_axis=0, tiled=True)

    src = lax.dynamic_slice_in_dim(relayout, s * rows, rows, 0) // rows
    before = jnp.arange(rows)[None, :] < jnp.arange(rows)[:, None]
    nth = jnp.sum((before & (src[None, :] == src[:, None])).astype(jnp.int32), axis=1)
    slot = src * chunk + nth
    per_dev = rows // (n_z * n_core)
    slot3 = slot.reshape(n_z, n_core, per_dev)
    cols = jnp.arange(rows, dtype=jnp.int32)[None, :]

    order = jnp.concatenate(
        [jnp.take(slot3, n_core - 1 - c, axis=1).reshape(-1), jnp.take(slot3, c, axis=1).reshape(-1)]
    )
    sel = (order[:, None] == cols).astype(jnp.bfloat16)
    relaid = jnp.dot(sel, arrived, preferred_element_type=jnp.float32).astype(jnp.bfloat16)
    part = jnp.dot(relaid, out_weight, preferred_element_type=jnp.float32).astype(jnp.bfloat16)
    share_rows = rows // n_core
    got = lax.ppermute(part[:share_rows], "core", perm=[(0, 1), (1, 0)])
    part_own = part[share_rows:]
    half = (part_own.astype(jnp.float32) + got.astype(jnp.float32)).astype(jnp.bfloat16)
    return lax.psum_scatter(half, "z", scatter_dimension=0, tiled=True)

def solution(mesh):
    n_seq, n_tp = mesh.devices.shape
    n_x = 4
    mesh4 = Mesh(mesh.devices.reshape(n_seq // n_x, n_x, n_tp // 2, 2), ("y", "x", "z", "core"))
    seq = ("y", "x")
    tp = ("z", "core")
    return jax.shard_map(
        shards,
        mesh=mesh4,
        in_specs=(
            P(),
            P(),
            P(seq, tp),
            P(seq + tp, None),
            P(seq + tp, None),
            P(tp, None),
        ),
        out_specs=P(seq + tp, None),
        check_vma=False,
    )
```

```python
import functools

import jax
import jax.numpy as jnp
import numpy as np
from jax import lax
from jax.experimental import pallas as pl
from jax.sharding import Mesh
from jax.sharding import PartitionSpec as P

QH = 32
KVH = 4
HD = 128
MOST_LEN = 2048


def _attention_body(scale, n_pieces, heads, carry_in, final, q_ref, *refs):
    kv_refs = refs[:n_pieces]
    refs = refs[n_pieces:]
    qp_ref, qs_ref, kp_ref, ks_ref = refs[:4]
    refs = refs[4:]
    if carry_in:
        m_in, l_in, acc_in = refs[:3]
        refs = refs[3:]
    qp = qp_ref[...]
    qs = qs_ref[...]
    lives = [(kp_ref[pl.ds(p, 1), :] <= qp) & (ks_ref[pl.ds(p, 1), :] == qs) for p in range(n_pieces)]
    for h in range(heads):
        q = q_ref[:, pl.ds(h * HD, HD)]
        scores = [
            jnp.where(
                lives[p],
                lax.dot_general(
                    q, kv_refs[p][:, pl.ds(0, HD)], (((1,), (1,)), ((), ())),
                    preferred_element_type=jnp.float32,
                ) * scale,
                jnp.float32(-1e30),
            )
            for p in range(n_pieces)
        ]
        peak = functools.reduce(jnp.maximum, [jnp.max(s, axis=1, keepdims=True) for s in scores])
        if carry_in:
            peak = jnp.maximum(peak, m_in[h])
        expos = [jnp.where(lives[p], jnp.exp(scores[p] - peak), jnp.float32(0.0)) for p in range(n_pieces)]
        denom = functools.reduce(jnp.add, [jnp.sum(e, axis=1, keepdims=True) for e in expos])
        summed = functools.reduce(
            jnp.add,
            [
                jnp.dot(expos[p].astype(jnp.bfloat16), kv_refs[p][:, pl.ds(HD, HD)], preferred_element_type=jnp.float32)
                for p in range(n_pieces)
            ],
        )
        if carry_in:
            alpha = jnp.exp(m_in[h] - peak)
            denom = denom + alpha * l_in[h]
            summed = summed + alpha * acc_in[:, pl.ds(h * HD, HD)]
        if final:
            refs[0][:, pl.ds(h * HD, HD)] = (summed / denom).astype(refs[0].dtype)
        else:
            refs[0][h] = peak
            refs[1][h] = denom
            refs[2][:, pl.ds(h * HD, HD)] = summed


def attention(q, pieces, q_pos, q_seg, k_pos, k_seg, scale, carry=None, final=True):
    rows, width = q.shape
    heads = width // HD
    n_pieces = len(pieces)
    n = pieces[0].shape[0]
    args = [q, *pieces, q_pos.reshape(rows, 1), q_seg.reshape(rows, 1), k_pos, k_seg]
    if carry is not None:
        args += list(carry)
    if final:
        out_shape = jax.ShapeDtypeStruct((rows, width), jnp.bfloat16)
    else:
        out_shape = [
            jax.ShapeDtypeStruct((heads, rows, 1), jnp.float32),
            jax.ShapeDtypeStruct((heads, rows, 1), jnp.float32),
            jax.ShapeDtypeStruct((rows, width), jnp.float32),
        ]
    return pl.pallas_call(
        functools.partial(_attention_body, scale, n_pieces, heads, carry is not None, final),
        out_shape=out_shape,
        cost_estimate=pl.CostEstimate(
            flops=4 * rows * n * n_pieces * HD * heads,
            transcendentals=rows * n * n_pieces * heads,
            bytes_accessed=2 * (2 * rows * width + 2 * n_pieces * n * HD),
        ),
    )(*args)


def shards(segment_ids, relayout, queries, keys, values, out_weight):
    rows = queries.shape[0]
    n_seq = lax.axis_size("y") * lax.axis_size("x")
    n_z = lax.axis_size("z")
    n_core = lax.axis_size("core")
    s = lax.axis_index("y") * lax.axis_size("x") + lax.axis_index("x")
    t = lax.axis_index("z") * n_core + lax.axis_index("core")
    heads_here = queries.shape[1] // HD
    group = QH // KVH
    kv_width = keys.shape[1]
    scale = HD ** (-0.5)
    back = -(-(MOST_LEN - 1) // rows)
    back = min(back, n_seq - 1)

    n_tp = n_z * n_core
    kv_heads = kv_width // HD
    n_x = lax.axis_size("x")
    share = group // heads_here
    assert n_tp == kv_heads * share
    k_h = jnp.transpose(keys.reshape(keys.shape[0], kv_heads, HD), (1, 0, 2))
    v_h = jnp.transpose(values.reshape(values.shape[0], kv_heads, HD), (1, 0, 2))
    kv_h = jnp.concatenate([k_h, v_h], axis=2)
    pieces = jnp.broadcast_to(
        kv_h[None, :, None], (n_x, kv_heads, share) + kv_h.shape[1:]
    ).reshape((n_x * n_tp,) + kv_h.shape[1:])
    row = lax.all_to_all(pieces, ("x", "z", "core"), split_axis=0, concat_axis=0, tiled=True)
    row = row.reshape(n_x * rows, 2 * HD)

    n_y = lax.axis_size("y")
    x = lax.axis_index("x")
    c = lax.axis_index("core")
    rows_back = -(-back // n_x)
    assert rows_back == n_core
    perm = []
    for cc in range(n_core):
        k = cc + 1
        if k <= rows_back:
            perm += [(yy * n_core + cc, (yy + k) * n_core + cc) for yy in range(n_y - k)]
    fetched = lax.ppermute(row, ("y", "core"), perm=perm)
    y = lax.axis_index("y")
    span = n_x * rows
    piece_rows = [y - 1 - c, y - n_core + c, y]
    k_pos = jnp.stack([r * span + jnp.arange(span, dtype=jnp.int32) for r in piece_rows])
    pad = rows_back * span
    seg_pad = jnp.concatenate([jnp.full((pad,), -1, jnp.int32), segment_ids])
    k_seg = jnp.stack([lax.dynamic_slice_in_dim(seg_pad, r * span + pad, span, 0) for r in piece_rows])
    q_pos = s * rows + jnp.arange(rows, dtype=jnp.int32)
    q_seg = lax.dynamic_slice_in_dim(segment_ids, s * rows, rows, 0)
    chunk = rows // n_seq
    total = relayout.shape[0]
    here = s * rows + jnp.arange(rows, dtype=jnp.int32)
    new_of = jnp.sum(
        jnp.where(relayout[None, :] == here[:, None], jnp.arange(total, dtype=jnp.int32)[None, :], 0),
        axis=1,
    )
    rank = jnp.sum((new_of[None, :] < new_of[:, None]).astype(jnp.int32), axis=1)
    send_hit = rank[None, :] == jnp.arange(rows, dtype=jnp.int32)[:, None]
    q_sent = jnp.dot(send_hit.astype(jnp.bfloat16), queries, preferred_element_type=jnp.float32).astype(jnp.bfloat16)
    q_pos = jnp.sum(jnp.where(send_hit, here[None, :], 0), axis=1)
    q_seg = jnp.sum(jnp.where(send_hit, q_seg[None, :], 0), axis=1)
    carry = attention(q_sent, [row], q_pos, q_seg, k_pos[2:], k_seg[2:], scale, final=False)
    fetched, carry = lax.optimization_barrier((fetched, carry))
    swapped = lax.ppermute(fetched, "core", perm=[(i, (i + 1) % n_core) for i in range(n_core)])
    to_send = attention(
        q_sent, [fetched, swapped], q_pos, q_seg, k_pos[:2], k_seg[:2], scale, carry=carry
    )

    arrived = lax.all_to_all(to_send, ("y", "x"), split_axis=0, concat_axis=0, tiled=True)

    src = lax.dynamic_slice_in_dim(relayout, s * rows, rows, 0) // rows
    before = jnp.arange(rows)[None, :] < jnp.arange(rows)[:, None]
    nth = jnp.sum((before & (src[None, :] == src[:, None])).astype(jnp.int32), axis=1)
    slot = src * chunk + nth
    per_dev = rows // (n_z * n_core)
    slot3 = slot.reshape(n_z, n_core, per_dev)
    cols = jnp.arange(rows, dtype=jnp.int32)[None, :]
    swap_pairs = [(i, (i + 1) % n_core) for i in range(n_core)]
    w_pair = jnp.concatenate([out_weight, lax.ppermute(out_weight, "core", perm=swap_pairs)], axis=0)
    both = jnp.concatenate([arrived, lax.ppermute(arrived, "core", perm=swap_pairs)], axis=1)
    mine = jnp.take(slot3, c, axis=1).reshape(-1)
    sel = (mine[:, None] == cols).astype(jnp.bfloat16)
    relaid = jnp.dot(sel, both, preferred_element_type=jnp.float32).astype(jnp.bfloat16)
    half = jnp.dot(relaid, w_pair, preferred_element_type=jnp.float32).astype(jnp.bfloat16)
    return lax.psum_scatter(half, "z", scatter_dimension=0, tiled=True)

def solution(mesh):
    n_seq, n_tp = mesh.devices.shape
    n_x = 4
    mesh4 = Mesh(mesh.devices.reshape(n_seq // n_x, n_x, n_tp // 2, 2), ("y", "x", "z", "core"))
    seq = ("y", "x")
    tp = ("z", "core")
    return jax.shard_map(
        shards,
        mesh=mesh4,
        in_specs=(
            P(),
            P(),
            P(seq, tp),
            P(seq + tp, None),
            P(seq + tp, None),
            P(tp, None),
        ),
        out_specs=P(seq + tp, None),
        check_vma=False,
    )
```

```python
import functools

import jax
import jax.numpy as jnp
import numpy as np
from jax import lax
from jax.experimental import pallas as pl
from jax.sharding import Mesh
from jax.sharding import PartitionSpec as P

QH = 32
KVH = 4
HD = 128
MOST_LEN = 2048


def _attention_body(scale, n_pieces, heads, carry_in, final, q_ref, *refs):
    kv_refs = refs[:n_pieces]
    refs = refs[n_pieces:]
    qp_ref, qs_ref, kp_ref, ks_ref = refs[:4]
    refs = refs[4:]
    if carry_in:
        m_in, l_in, acc_in = refs[:3]
        refs = refs[3:]
    qp = qp_ref[...]
    qs = qs_ref[...]
    lives = [(kp_ref[pl.ds(p, 1), :] <= qp) & (ks_ref[pl.ds(p, 1), :] == qs) for p in range(n_pieces)]
    for h in range(heads):
        q = q_ref[:, pl.ds(h * HD, HD)]
        scores = [
            jnp.where(
                lives[p],
                lax.dot_general(
                    q, kv_refs[p][:, pl.ds(0, HD)], (((1,), (1,)), ((), ())),
                    preferred_element_type=jnp.float32,
                ) * scale,
                jnp.float32(-1e30),
            )
            for p in range(n_pieces)
        ]
        peak = functools.reduce(jnp.maximum, [jnp.max(s, axis=1, keepdims=True) for s in scores])
        if carry_in:
            peak = jnp.maximum(peak, m_in[h])
        expos = [jnp.where(lives[p], jnp.exp(scores[p] - peak), jnp.float32(0.0)) for p in range(n_pieces)]
        denom = functools.reduce(jnp.add, [jnp.sum(e, axis=1, keepdims=True) for e in expos])
        summed = functools.reduce(
            jnp.add,
            [
                jnp.dot(expos[p].astype(jnp.bfloat16), kv_refs[p][:, pl.ds(HD, HD)], preferred_element_type=jnp.float32)
                for p in range(n_pieces)
            ],
        )
        if carry_in:
            alpha = jnp.exp(m_in[h] - peak)
            denom = denom + alpha * l_in[h]
            summed = summed + alpha * acc_in[:, pl.ds(h * HD, HD)]
        if final:
            refs[0][:, pl.ds(h * HD, HD)] = (summed / denom).astype(refs[0].dtype)
        else:
            refs[0][h] = peak
            refs[1][h] = denom
            refs[2][:, pl.ds(h * HD, HD)] = summed


def attention(q, pieces, q_pos, q_seg, k_pos, k_seg, scale, carry=None, final=True):
    rows, width = q.shape
    heads = width // HD
    n_pieces = len(pieces)
    n = pieces[0].shape[0]
    args = [q, *pieces, q_pos.reshape(rows, 1), q_seg.reshape(rows, 1), k_pos, k_seg]
    if carry is not None:
        args += list(carry)
    if final:
        out_shape = jax.ShapeDtypeStruct((rows, width), jnp.bfloat16)
    else:
        out_shape = [
            jax.ShapeDtypeStruct((heads, rows, 1), jnp.float32),
            jax.ShapeDtypeStruct((heads, rows, 1), jnp.float32),
            jax.ShapeDtypeStruct((rows, width), jnp.float32),
        ]
    return pl.pallas_call(
        functools.partial(_attention_body, scale, n_pieces, heads, carry is not None, final),
        out_shape=out_shape,
        cost_estimate=pl.CostEstimate(
            flops=4 * rows * n * n_pieces * HD * heads,
            transcendentals=rows * n * n_pieces * heads,
            bytes_accessed=2 * (2 * rows * width + 2 * n_pieces * n * HD),
        ),
    )(*args)


def shards(segment_ids, relayout, queries, keys, values, out_weight):
    rows = queries.shape[0]
    n_seq = lax.axis_size("y") * lax.axis_size("x")
    n_z = lax.axis_size("z")
    n_core = lax.axis_size("core")
    s = lax.axis_index("y") * lax.axis_size("x") + lax.axis_index("x")
    t = lax.axis_index("z") * n_core + lax.axis_index("core")
    heads_here = queries.shape[1] // HD
    group = QH // KVH
    kv_width = keys.shape[1]
    scale = HD ** (-0.5)
    back = -(-(MOST_LEN - 1) // rows)
    back = min(back, n_seq - 1)

    n_tp = n_z * n_core
    kv_heads = kv_width // HD
    n_x = lax.axis_size("x")
    share = group // heads_here
    assert n_tp == kv_heads * share
    k_h = jnp.transpose(keys.reshape(keys.shape[0], kv_heads, HD), (1, 0, 2))
    v_h = jnp.transpose(values.reshape(values.shape[0], kv_heads, HD), (1, 0, 2))
    kv_h = jnp.concatenate([k_h, v_h], axis=2)
    pieces = jnp.broadcast_to(
        kv_h[None, :, None], (n_x, kv_heads, n_z // kv_heads) + kv_h.shape[1:]
    ).reshape((n_x * n_z,) + kv_h.shape[1:])
    mine = lax.all_to_all(pieces, ("x", "z"), split_axis=0, concat_axis=0, tiled=True)
    other = lax.ppermute(mine, "core", perm=[(i, (i + 1) % n_core) for i in range(n_core)])
    row = jnp.stack([mine.reshape(n_x, n_z, -1, 2 * HD), other.reshape(n_x, n_z, -1, 2 * HD)], axis=2)
    row = row.reshape(n_x * rows, 2 * HD)

    n_y = lax.axis_size("y")
    x = lax.axis_index("x")
    c = lax.axis_index("core")
    rows_back = -(-back // n_x)
    assert rows_back == n_core
    perm = []
    for cc in range(n_core):
        k = cc + 1
        if k <= rows_back:
            perm += [(yy * n_core + cc, (yy + k) * n_core + cc) for yy in range(n_y - k)]
    fetched = lax.ppermute(row, ("y", "core"), perm=perm)
    y = lax.axis_index("y")
    span = n_x * rows
    piece_rows = [y - 1 - c, y - n_core + c, y]
    makers = [c, n_core - 1 - c, c]

    def in_order(vec, p):
        v = vec.reshape(n_x, n_z, n_core, -1)
        return jnp.where(p == 0, v, v[:, :, ::-1, :]).reshape(-1)

    k_pos = jnp.stack(
        [in_order(r * span + jnp.arange(span, dtype=jnp.int32), p) for r, p in zip(piece_rows, makers)]
    )
    pad = rows_back * span
    seg_pad = jnp.concatenate([jnp.full((pad,), -1, jnp.int32), segment_ids])
    k_seg = jnp.stack(
        [in_order(lax.dynamic_slice_in_dim(seg_pad, r * span + pad, span, 0), p) for r, p in zip(piece_rows, makers)]
    )
    q_pos = s * rows + jnp.arange(rows, dtype=jnp.int32)
    q_seg = lax.dynamic_slice_in_dim(segment_ids, s * rows, rows, 0)
    chunk = rows // n_seq
    total = relayout.shape[0]
    here = s * rows + jnp.arange(rows, dtype=jnp.int32)
    new_of = jnp.sum(
        jnp.where(relayout[None, :] == here[:, None], jnp.arange(total, dtype=jnp.int32)[None, :], 0),
        axis=1,
    )
    rank = jnp.sum((new_of[None, :] < new_of[:, None]).astype(jnp.int32), axis=1)
    send_hit = rank[None, :] == jnp.arange(rows, dtype=jnp.int32)[:, None]
    q_sent = jnp.dot(send_hit.astype(jnp.bfloat16), queries, preferred_element_type=jnp.float32).astype(jnp.bfloat16)
    q_pos = jnp.sum(jnp.where(send_hit, here[None, :], 0), axis=1)
    q_seg = jnp.sum(jnp.where(send_hit, q_seg[None, :], 0), axis=1)
    carry = attention(q_sent, [row], q_pos, q_seg, k_pos[2:], k_seg[2:], scale, final=False)
    fetched, carry = lax.optimization_barrier((fetched, carry))
    swapped = lax.ppermute(fetched, "core", perm=[(i, (i + 1) % n_core) for i in range(n_core)])
    to_send = attention(
        q_sent, [fetched, swapped], q_pos, q_seg, k_pos[:2], k_seg[:2], scale, carry=carry
    )

    arrived = lax.all_to_all(to_send, ("y", "x"), split_axis=0, concat_axis=0, tiled=True)

    src = lax.dynamic_slice_in_dim(relayout, s * rows, rows, 0) // rows
    before = jnp.arange(rows)[None, :] < jnp.arange(rows)[:, None]
    nth = jnp.sum((before & (src[None, :] == src[:, None])).astype(jnp.int32), axis=1)
    slot = src * chunk + nth
    per_dev = rows // (n_z * n_core)
    slot3 = slot.reshape(n_z, n_core, per_dev)
    cols = jnp.arange(rows, dtype=jnp.int32)[None, :]
    swap_pairs = [(i, (i + 1) % n_core) for i in range(n_core)]
    w_pair = jnp.concatenate([out_weight, lax.ppermute(out_weight, "core", perm=swap_pairs)], axis=0)
    both = jnp.concatenate([arrived, lax.ppermute(arrived, "core", perm=swap_pairs)], axis=1)
    mine = jnp.take(slot3, c, axis=1).reshape(-1)
    sel = (mine[:, None] == cols).astype(jnp.bfloat16)
    relaid = jnp.dot(sel, both, preferred_element_type=jnp.float32).astype(jnp.bfloat16)
    half = jnp.dot(relaid, w_pair, preferred_element_type=jnp.float32).astype(jnp.bfloat16)
    return lax.psum_scatter(half, "z", scatter_dimension=0, tiled=True)

def solution(mesh):
    n_seq, n_tp = mesh.devices.shape
    n_x = 4
    mesh4 = Mesh(mesh.devices.reshape(n_seq // n_x, n_x, n_tp // 2, 2), ("y", "x", "z", "core"))
    seq = ("y", "x")
    tp = ("z", "core")
    return jax.shard_map(
        shards,
        mesh=mesh4,
        in_specs=(
            P(),
            P(),
            P(seq, tp),
            P(seq + tp, None),
            P(seq + tp, None),
            P(tp, None),
        ),
        out_specs=P(seq + tp, None),
        check_vma=False,
    )
```

```python
import functools

import jax
import jax.numpy as jnp
import numpy as np
from jax import lax
from jax.experimental import pallas as pl
from jax.sharding import Mesh
from jax.sharding import PartitionSpec as P

QH = 32
KVH = 4
HD = 128
MOST_LEN = 2048


def _attention_body(scale, n_pieces, heads, carry_in, final, q_ref, *refs):
    kv_refs = refs[:n_pieces]
    refs = refs[n_pieces:]
    qp_ref, qs_ref, kp_ref, ks_ref = refs[:4]
    refs = refs[4:]
    if carry_in:
        m_in, l_in, acc_in = refs[:3]
        refs = refs[3:]
    qp = qp_ref[...]
    qs = qs_ref[...]
    lives = [(kp_ref[pl.ds(p, 1), :] <= qp) & (ks_ref[pl.ds(p, 1), :] == qs) for p in range(n_pieces)]
    for h in range(heads):
        q = q_ref[:, pl.ds(h * HD, HD)]
        scores = [
            jnp.where(
                lives[p],
                lax.dot_general(
                    q, kv_refs[p][:, pl.ds(0, HD)], (((1,), (1,)), ((), ())),
                    preferred_element_type=jnp.float32,
                ) * scale,
                jnp.float32(-1e30),
            )
            for p in range(n_pieces)
        ]
        peak = functools.reduce(jnp.maximum, [jnp.max(s, axis=1, keepdims=True) for s in scores])
        if carry_in:
            peak = jnp.maximum(peak, m_in[h])
        expos = [jnp.where(lives[p], jnp.exp(scores[p] - peak), jnp.float32(0.0)) for p in range(n_pieces)]
        denom = functools.reduce(jnp.add, [jnp.sum(e, axis=1, keepdims=True) for e in expos])
        summed = functools.reduce(
            jnp.add,
            [
                jnp.dot(expos[p].astype(jnp.bfloat16), kv_refs[p][:, pl.ds(HD, HD)], preferred_element_type=jnp.float32)
                for p in range(n_pieces)
            ],
        )
        if carry_in:
            alpha = jnp.exp(m_in[h] - peak)
            denom = denom + alpha * l_in[h]
            summed = summed + alpha * acc_in[:, pl.ds(h * HD, HD)]
        if final:
            refs[0][:, pl.ds(h * HD, HD)] = (summed / denom).astype(refs[0].dtype)
        else:
            refs[0][h] = peak
            refs[1][h] = denom
            refs[2][:, pl.ds(h * HD, HD)] = summed


def attention(q, pieces, q_pos, q_seg, k_pos, k_seg, scale, carry=None, final=True):
    rows, width = q.shape
    heads = width // HD
    n_pieces = len(pieces)
    n = pieces[0].shape[0]
    args = [q, *pieces, q_pos.reshape(rows, 1), q_seg.reshape(rows, 1), k_pos, k_seg]
    if carry is not None:
        args += list(carry)
    if final:
        out_shape = jax.ShapeDtypeStruct((rows, width), jnp.bfloat16)
    else:
        out_shape = [
            jax.ShapeDtypeStruct((heads, rows, 1), jnp.float32),
            jax.ShapeDtypeStruct((heads, rows, 1), jnp.float32),
            jax.ShapeDtypeStruct((rows, width), jnp.float32),
        ]
    return pl.pallas_call(
        functools.partial(_attention_body, scale, n_pieces, heads, carry is not None, final),
        out_shape=out_shape,
        cost_estimate=pl.CostEstimate(
            flops=4 * rows * n * n_pieces * HD * heads,
            transcendentals=rows * n * n_pieces * heads,
            bytes_accessed=2 * (2 * rows * width + 2 * n_pieces * n * HD),
        ),
    )(*args)


def shards(segment_ids, relayout, queries, keys, values, out_weight):
    rows = queries.shape[0]
    n_seq = lax.axis_size("y") * lax.axis_size("x")
    n_z = lax.axis_size("z")
    n_core = lax.axis_size("core")
    s = lax.axis_index("y") * lax.axis_size("x") + lax.axis_index("x")
    t = lax.axis_index("z") * n_core + lax.axis_index("core")
    heads_here = queries.shape[1] // HD
    group = QH // KVH
    kv_width = keys.shape[1]
    scale = HD ** (-0.5)
    back = -(-(MOST_LEN - 1) // rows)
    back = min(back, n_seq - 1)

    n_tp = n_z * n_core
    kv_heads = kv_width // HD
    n_x = lax.axis_size("x")
    share = group // heads_here
    assert n_tp == kv_heads * share
    k_h = jnp.transpose(keys.reshape(keys.shape[0], kv_heads, HD), (1, 0, 2))
    v_h = jnp.transpose(values.reshape(values.shape[0], kv_heads, HD), (1, 0, 2))
    kv_h = jnp.concatenate([k_h, v_h], axis=2)
    pieces = jnp.broadcast_to(
        kv_h[None, :, None], (n_x, kv_heads, n_z // kv_heads) + kv_h.shape[1:]
    ).reshape((n_x * n_z,) + kv_h.shape[1:])
    mine = lax.all_to_all(pieces, ("x", "z"), split_axis=0, concat_axis=0, tiled=True)
    mine, w_late = lax.optimization_barrier((mine, out_weight))
    other = lax.ppermute(mine, "core", perm=[(i, (i + 1) % n_core) for i in range(n_core)])
    row = jnp.stack([mine.reshape(n_x, n_z, -1, 2 * HD), other.reshape(n_x, n_z, -1, 2 * HD)], axis=2)
    row = row.reshape(n_x * rows, 2 * HD)

    n_y = lax.axis_size("y")
    x = lax.axis_index("x")
    c = lax.axis_index("core")
    rows_back = -(-back // n_x)
    assert rows_back == n_core
    perm = []
    for cc in range(n_core):
        k = cc + 1
        if k <= rows_back:
            perm += [(yy * n_core + cc, (yy + k) * n_core + cc) for yy in range(n_y - k)]
    fetched = lax.ppermute(row, ("y", "core"), perm=perm)
    y = lax.axis_index("y")
    span = n_x * rows
    piece_rows = [y - 1 - c, y - n_core + c, y]
    makers = [c, n_core - 1 - c, c]

    def in_order(vec, p):
        v = vec.reshape(n_x, n_z, n_core, -1)
        return jnp.where(p == 0, v, v[:, :, ::-1, :]).reshape(-1)

    k_pos = jnp.stack(
        [in_order(r * span + jnp.arange(span, dtype=jnp.int32), p) for r, p in zip(piece_rows, makers)]
    )
    pad = rows_back * span
    seg_pad = jnp.concatenate([jnp.full((pad,), -1, jnp.int32), segment_ids])
    k_seg = jnp.stack(
        [in_order(lax.dynamic_slice_in_dim(seg_pad, r * span + pad, span, 0), p) for r, p in zip(piece_rows, makers)]
    )
    q_pos = s * rows + jnp.arange(rows, dtype=jnp.int32)
    q_seg = lax.dynamic_slice_in_dim(segment_ids, s * rows, rows, 0)
    chunk = rows // n_seq
    total = relayout.shape[0]
    here = s * rows + jnp.arange(rows, dtype=jnp.int32)
    new_of = jnp.sum(
        jnp.where(relayout[None, :] == here[:, None], jnp.arange(total, dtype=jnp.int32)[None, :], 0),
        axis=1,
    )
    rank = jnp.sum((new_of[None, :] < new_of[:, None]).astype(jnp.int32), axis=1)
    send_hit = rank[None, :] == jnp.arange(rows, dtype=jnp.int32)[:, None]
    q_sent = jnp.dot(send_hit.astype(jnp.bfloat16), queries, preferred_element_type=jnp.float32).astype(jnp.bfloat16)
    q_pos = jnp.sum(jnp.where(send_hit, here[None, :], 0), axis=1)
    q_seg = jnp.sum(jnp.where(send_hit, q_seg[None, :], 0), axis=1)
    carry = attention(q_sent, [row], q_pos, q_seg, k_pos[2:], k_seg[2:], scale, final=False)
    fetched, carry = lax.optimization_barrier((fetched, carry))
    swapped = lax.ppermute(fetched, "core", perm=[(i, (i + 1) % n_core) for i in range(n_core)])
    to_send = attention(
        q_sent, [fetched, swapped], q_pos, q_seg, k_pos[:2], k_seg[:2], scale, carry=carry
    )

    arrived = lax.all_to_all(to_send, ("y", "x"), split_axis=0, concat_axis=0, tiled=True)

    src = lax.dynamic_slice_in_dim(relayout, s * rows, rows, 0) // rows
    before = jnp.arange(rows)[None, :] < jnp.arange(rows)[:, None]
    nth = jnp.sum((before & (src[None, :] == src[:, None])).astype(jnp.int32), axis=1)
    slot = src * chunk + nth
    per_dev = rows // (n_z * n_core)
    slot3 = slot.reshape(n_z, n_core, per_dev)
    cols = jnp.arange(rows, dtype=jnp.int32)[None, :]
    swap_pairs = [(i, (i + 1) % n_core) for i in range(n_core)]
    w_pair = jnp.concatenate([out_weight, lax.ppermute(w_late, "core", perm=swap_pairs)], axis=0)
    both = jnp.concatenate([arrived, lax.ppermute(arrived, "core", perm=swap_pairs)], axis=1)
    mine = jnp.take(slot3, c, axis=1).reshape(-1)
    sel = (mine[:, None] == cols).astype(jnp.bfloat16)
    relaid = jnp.dot(sel, both, preferred_element_type=jnp.float32).astype(jnp.bfloat16)
    half = jnp.dot(relaid, w_pair, preferred_element_type=jnp.float32).astype(jnp.bfloat16)
    return lax.psum_scatter(half, "z", scatter_dimension=0, tiled=True)

def solution(mesh):
    n_seq, n_tp = mesh.devices.shape
    n_x = 4
    mesh4 = Mesh(mesh.devices.reshape(n_seq // n_x, n_x, n_tp // 2, 2), ("y", "x", "z", "core"))
    seq = ("y", "x")
    tp = ("z", "core")
    return jax.shard_map(
        shards,
        mesh=mesh4,
        in_specs=(
            P(),
            P(),
            P(seq, tp),
            P(seq + tp, None),
            P(seq + tp, None),
            P(tp, None),
        ),
        out_specs=P(seq + tp, None),
        check_vma=False,
    )
```

```python
import functools

import jax
import jax.numpy as jnp
import numpy as np
from jax import lax
from jax.experimental import pallas as pl
from jax.sharding import Mesh
from jax.sharding import PartitionSpec as P

QH = 32
KVH = 4
HD = 128
MOST_LEN = 2048


def _attention_body(scale, n_pieces, heads, carry_in, final, q_ref, *refs):
    kv_refs = refs[:n_pieces]
    refs = refs[n_pieces:]
    qp_ref, qs_ref, kp_ref, ks_ref = refs[:4]
    refs = refs[4:]
    if carry_in:
        m_in, l_in, acc_in = refs[:3]
        refs = refs[3:]
    qp = qp_ref[...]
    qs = qs_ref[...]
    lives = [(kp_ref[pl.ds(p, 1), :] <= qp) & (ks_ref[pl.ds(p, 1), :] == qs) for p in range(n_pieces)]
    for h in range(heads):
        q = q_ref[:, pl.ds(h * HD, HD)]
        scores = [
            jnp.where(
                lives[p],
                lax.dot_general(
                    q, kv_refs[p][:, pl.ds(0, HD)], (((1,), (1,)), ((), ())),
                    preferred_element_type=jnp.float32,
                ) * scale,
                jnp.float32(-1e30),
            )
            for p in range(n_pieces)
        ]
        peak = functools.reduce(jnp.maximum, [jnp.max(s, axis=1, keepdims=True) for s in scores])
        if carry_in:
            peak = jnp.maximum(peak, m_in[h])
        expos = [jnp.where(lives[p], jnp.exp(scores[p] - peak), jnp.float32(0.0)) for p in range(n_pieces)]
        denom = functools.reduce(jnp.add, [jnp.sum(e, axis=1, keepdims=True) for e in expos])
        summed = functools.reduce(
            jnp.add,
            [
                jnp.dot(expos[p].astype(jnp.bfloat16), kv_refs[p][:, pl.ds(HD, HD)], preferred_element_type=jnp.float32)
                for p in range(n_pieces)
            ],
        )
        if carry_in:
            alpha = jnp.exp(m_in[h] - peak)
            denom = denom + alpha * l_in[h]
            summed = summed + alpha * acc_in[:, pl.ds(h * HD, HD)]
        if final:
            refs[0][:, pl.ds(h * HD, HD)] = (summed / denom).astype(refs[0].dtype)
        else:
            refs[0][h] = peak
            refs[1][h] = denom
            refs[2][:, pl.ds(h * HD, HD)] = summed


def attention(q, pieces, q_pos, q_seg, k_pos, k_seg, scale, carry=None, final=True):
    rows, width = q.shape
    heads = width // HD
    n_pieces = len(pieces)
    n = pieces[0].shape[0]
    args = [q, *pieces, q_pos.reshape(rows, 1), q_seg.reshape(rows, 1), k_pos, k_seg]
    if carry is not None:
        args += list(carry)
    if final:
        out_shape = jax.ShapeDtypeStruct((rows, width), jnp.bfloat16)
    else:
        out_shape = [
            jax.ShapeDtypeStruct((heads, rows, 1), jnp.float32),
            jax.ShapeDtypeStruct((heads, rows, 1), jnp.float32),
            jax.ShapeDtypeStruct((rows, width), jnp.float32),
        ]
    return pl.pallas_call(
        functools.partial(_attention_body, scale, n_pieces, heads, carry is not None, final),
        out_shape=out_shape,
        cost_estimate=pl.CostEstimate(
            flops=4 * rows * n * n_pieces * HD * heads,
            transcendentals=rows * n * n_pieces * heads,
            bytes_accessed=2 * (2 * rows * width + 2 * n_pieces * n * HD),
        ),
    )(*args)


def shards(segment_ids, relayout, queries, keys, values, out_weight):
    rows = queries.shape[0]
    n_seq = lax.axis_size("y") * lax.axis_size("x")
    n_z = lax.axis_size("z")
    n_core = lax.axis_size("core")
    s = lax.axis_index("y") * lax.axis_size("x") + lax.axis_index("x")
    t = lax.axis_index("z") * n_core + lax.axis_index("core")
    heads_here = queries.shape[1] // HD
    group = QH // KVH
    kv_width = keys.shape[1]
    scale = HD ** (-0.5)
    back = -(-(MOST_LEN - 1) // rows)
    back = min(back, n_seq - 1)

    n_tp = n_z * n_core
    kv_heads = kv_width // HD
    n_x = lax.axis_size("x")
    share = group // heads_here
    assert n_tp == kv_heads * share
    k_h = jnp.transpose(keys.reshape(keys.shape[0], kv_heads, HD), (1, 0, 2))
    v_h = jnp.transpose(values.reshape(values.shape[0], kv_heads, HD), (1, 0, 2))
    kv_h = jnp.concatenate([k_h, v_h], axis=2)
    pieces = jnp.broadcast_to(
        kv_h[None, :, None], (n_x, kv_heads, n_z // kv_heads) + kv_h.shape[1:]
    ).reshape((n_x * n_z,) + kv_h.shape[1:])
    mine = lax.all_to_all(pieces, ("x", "z"), split_axis=0, concat_axis=0, tiled=True)
    other = lax.ppermute(mine, "core", perm=[(i, (i + 1) % n_core) for i in range(n_core)])
    row = jnp.stack([mine.reshape(n_x, n_z, -1, 2 * HD), other.reshape(n_x, n_z, -1, 2 * HD)], axis=2)
    row = row.reshape(n_x * rows, 2 * HD)

    n_y = lax.axis_size("y")
    x = lax.axis_index("x")
    c = lax.axis_index("core")
    rows_back = -(-back // n_x)
    assert rows_back == n_core
    perm = []
    for cc in range(n_core):
        k = cc + 1
        if k <= rows_back:
            perm += [(yy * n_core + cc, (yy + k) * n_core + cc) for yy in range(n_y - k)]
    fetched = lax.ppermute(row, ("y", "core"), perm=perm)
    y = lax.axis_index("y")
    span = n_x * rows
    piece_rows = [y - 1 - c, y - n_core + c, y]
    makers = [c, n_core - 1 - c, c]

    def in_order(vec, p):
        v = vec.reshape(n_x, n_z, n_core, -1)
        return jnp.where(p == 0, v, v[:, :, ::-1, :]).reshape(-1)

    k_pos = jnp.stack(
        [in_order(r * span + jnp.arange(span, dtype=jnp.int32), p) for r, p in zip(piece_rows, makers)]
    )
    pad = rows_back * span
    seg_pad = jnp.concatenate([jnp.full((pad,), -1, jnp.int32), segment_ids])
    k_seg = jnp.stack(
        [in_order(lax.dynamic_slice_in_dim(seg_pad, r * span + pad, span, 0), p) for r, p in zip(piece_rows, makers)]
    )
    q_pos = s * rows + jnp.arange(rows, dtype=jnp.int32)
    q_seg = lax.dynamic_slice_in_dim(segment_ids, s * rows, rows, 0)
    chunk = rows // n_seq
    total = relayout.shape[0]
    here = s * rows + jnp.arange(rows, dtype=jnp.int32)
    new_of = jnp.sum(
        jnp.where(relayout[None, :] == here[:, None], jnp.arange(total, dtype=jnp.int32)[None, :], 0),
        axis=1,
    )
    rank = jnp.sum((new_of[None, :] < new_of[:, None]).astype(jnp.int32), axis=1)
    send_hit = rank[None, :] == jnp.arange(rows, dtype=jnp.int32)[:, None]
    q_sent = jnp.dot(send_hit.astype(jnp.bfloat16), queries, preferred_element_type=jnp.float32).astype(jnp.bfloat16)
    q_pos = jnp.sum(jnp.where(send_hit, here[None, :], 0), axis=1)
    q_seg = jnp.sum(jnp.where(send_hit, q_seg[None, :], 0), axis=1)
    carry = attention(q_sent, [row], q_pos, q_seg, k_pos[2:], k_seg[2:], scale, final=False)
    fetched, carry, w_late = lax.optimization_barrier((fetched, carry, out_weight))
    swapped = lax.ppermute(fetched, "core", perm=[(i, (i + 1) % n_core) for i in range(n_core)])
    to_send = attention(
        q_sent, [fetched, swapped], q_pos, q_seg, k_pos[:2], k_seg[:2], scale, carry=carry
    )

    arrived = lax.all_to_all(to_send, ("y", "x"), split_axis=0, concat_axis=0, tiled=True)

    src = lax.dynamic_slice_in_dim(relayout, s * rows, rows, 0) // rows
    before = jnp.arange(rows)[None, :] < jnp.arange(rows)[:, None]
    nth = jnp.sum((before & (src[None, :] == src[:, None])).astype(jnp.int32), axis=1)
    slot = src * chunk + nth
    per_dev = rows // (n_z * n_core)
    slot3 = slot.reshape(n_z, n_core, per_dev)
    cols = jnp.arange(rows, dtype=jnp.int32)[None, :]
    swap_pairs = [(i, (i + 1) % n_core) for i in range(n_core)]
    w_pair = jnp.concatenate([out_weight, lax.ppermute(w_late, "core", perm=swap_pairs)], axis=0)
    both = jnp.concatenate([arrived, lax.ppermute(arrived, "core", perm=swap_pairs)], axis=1)
    mine = jnp.take(slot3, c, axis=1).reshape(-1)
    sel = (mine[:, None] == cols).astype(jnp.bfloat16)
    relaid = jnp.dot(sel, both, preferred_element_type=jnp.float32).astype(jnp.bfloat16)
    half = jnp.dot(relaid, w_pair, preferred_element_type=jnp.float32).astype(jnp.bfloat16)
    return lax.psum_scatter(half, "z", scatter_dimension=0, tiled=True)

def solution(mesh):
    n_seq, n_tp = mesh.devices.shape
    n_x = 4
    mesh4 = Mesh(mesh.devices.reshape(n_seq // n_x, n_x, n_tp // 2, 2), ("y", "x", "z", "core"))
    seq = ("y", "x")
    tp = ("z", "core")
    return jax.shard_map(
        shards,
        mesh=mesh4,
        in_specs=(
            P(),
            P(),
            P(seq, tp),
            P(seq + tp, None),
            P(seq + tp, None),
            P(tp, None),
        ),
        out_specs=P(seq + tp, None),
        check_vma=False,
    )
```
